32 devices in a mesh: dom: 4 (over y, x), orb: 8 (over z, core).
Axes of the slice: x: 2, y: 2, z: 4, core: 2. Of those that a mesh axis runs over, the one named last changes fastest.
Arguments:
- orbitals: float32 [16, 24, 32, 256], P('orb', 'dom'), may hold values from -12 to 12
- potential: float32 [24, 32, 256], P('dom'), may hold values from 0 to 3
- degrees: int32 [8], P('orb'), may hold values from 1 to 3
Outputs:
- filtered: bfloat16 [16, 24, 32, 256], P('orb', 'dom')
- correlation: float32 [16, 16], P('orb')
The draws below stay inside these ranges and needn't reach their ends.
All inputs are finite; a program needn't handle non-finite values.
Results may differ from the reference program's by a relative error of at most 0.0004.
Values may be sent and summed in bfloat16 or wider, within the bound.
No kernel may reach another device: no remote copies, remote signals or barrier semaphores. Data moves between devices by JAX's collectives and lax.ppermute only.
A program may use at most 64 MiB of HBM per device.

```python
import jax
import jax.numpy as jnp
from jax import lax

NY = 32
NZ = 256
ORB_DEV = 2
DEG_MAX = 3
NX = 24
BLOCKS = 8
ORBS = 16


def draw_orbitals(key, part):
    key_noise, key_shared, key_scale = jax.random.split(key, 3)
    shape = (ORBS, NX, NY, NZ)
    noise = jnp.clip(jax.random.normal(key_noise, shape, jnp.float32), -5.0, 5.0)
    shared = jnp.clip(jax.random.normal(key_shared, (1, NX, NY, NZ), jnp.float32), -5.0, 5.0)
    scales = jax.random.uniform(key_scale, (ORBS, 1, 1, 1), jnp.float32, 0.5, 1.5)
    return scales * (noise + 0.6 * shared)


def set_ends(array, key, smallest, top_value):
    longest = array.shape.index(max(array.shape))
    spots = []
    for shift in (0, 1):
        where = [jax.random.randint(jax.random.fold_in(key, axis), (), 0, length) for axis, length in enumerate(array.shape)]
        where[longest] = (where[longest] + shift) % array.shape[longest]
        spots.append(tuple(where))
    return array.at[spots[0]].set(smallest).at[spots[1]].set(top_value)


def level_of(stream_key, shape, shards, low, largest):
    gain, own = 1.0, jax.random.fold_in(stream_key, 6)
    for position, blocks in shards:
        steps = jnp.exp(jax.random.uniform(jax.random.fold_in(own, position), (blocks,), jnp.float32, low / len(shards), largest / len(shards)))
        gain = gain * jnp.repeat(steps, shape[position] // blocks).reshape([-1 if axis == position else 1 for axis in range(len(shape))])
    return gain


def setup_inputs(seed: int = 0) -> dict:
    streams_of = jax.random.split(jax.random.key(seed), 4)
    orbitals = draw_orbitals(jax.random.fold_in(streams_of[3], 71), 0)
    potential = jnp.clip(3.0 * jax.random.uniform(streams_of[1], (NX, NY, NZ), jnp.float32) ** level_of(streams_of[1], (NX, NY, NZ), ((0, 4),), -0.2, 0.2), 0.0, 3.0)
    degrees = set_ends(jax.random.randint(streams_of[2], (BLOCKS,), 1, DEG_MAX + 1), jax.random.fold_in(streams_of[2], 1), 1, DEG_MAX).astype(jnp.int32)
    return dict(orbitals=orbitals, potential=potential, degrees=degrees)


CENTER_COEF = -5369.0 / 1800.0
STENCIL = (12.0 / 7.0, -15.0 / 56.0, 10.0 / 189.0, -1.0 / 112.0, 2.0 / 1925.0, -1.0 / 16632.0)
SHIFT_C = 8.5
HALF_W = 4.5


def hamiltonian(field, padded, potential):
    planes = field.shape[1]
    laplace = (3.0 * CENTER_COEF) * field
    for offset, weight in enumerate(STENCIL, 1):
        beside_all = padded[:, 6 + offset:6 + offset + planes] + padded[:, 6 - offset:6 - offset + planes]
        beside_all = beside_all + jnp.roll(field, offset, 2) + jnp.roll(field, -offset, 2)
        beside_all = beside_all + jnp.roll(field, offset, 3) + jnp.roll(field, -offset, 3)
        laplace = laplace + weight * beside_all
    return -0.5 * laplace + potential * field


def pad_zero(field):
    return jnp.pad(field, ((0, 0), (6, 6), (0, 0), (0, 0)))


def chebyshev(start, degree, potential):
    first = (hamiltonian(start, pad_zero(start), potential) - SHIFT_C * start) / HALF_W
    previous, current, picked = start, first, first
    for order in range(2, DEG_MAX + 1):
        following = 2.0 * (hamiltonian(current, pad_zero(current), potential) - SHIFT_C * current) / HALF_W - previous
        picked = jnp.where(degree >= order, following, picked)
        previous, current = current, following
    return picked


def reference(orbitals, potential, degrees):
    per_orbital = jnp.repeat(degrees, ORB_DEV)

    def one_orbital(pair):
        single, degree = pair
        return chebyshev(single[None], degree, potential)[0].astype(jnp.bfloat16)

    filtered = lax.map(one_orbital, (orbitals, per_orbital))
    flattened = filtered.reshape(ORBS, NX * NY * NZ)
    correlation = jnp.dot(flattened, flattened.T, preferred_element_type=jnp.float32) / float(NX * NY * NZ)
    return filtered, correlation
```

```python
import jax
import jax.numpy as jnp
from jax import lax
from jax.sharding import PartitionSpec as P

DEG_MAX = 3


CENTER_COEF = -5369.0 / 1800.0
STENCIL = (12.0 / 7.0, -15.0 / 56.0, 10.0 / 189.0, -1.0 / 112.0, 2.0 / 1925.0, -1.0 / 16632.0)
SHIFT_C = 8.5
HALF_W = 4.5


def with_halo(cells, sides, width):
    for axis, dim in sides:
        count = lax.axis_size(axis)
        ends = count - 1
        head = lax.slice_in_dim(cells, 0, width, axis=dim)
        tail = lax.slice_in_dim(cells, cells.shape[dim] - width, cells.shape[dim], axis=dim)
        cells = jnp.concatenate(
            [
                lax.ppermute(tail, axis, [(i, (i + 1) % count) for i in range(ends)]),
                cells,
                lax.ppermute(head, axis, [((i + 1) % count, i) for i in range(ends)]),
            ],
            axis=dim,
        )
    return cells


def hamiltonian(field, potential):
    padded = with_halo(field, (("dom", 1),), 6)
    planes = field.shape[1]
    laplace = 3.0 * CENTER_COEF * field
    for offset, weight in enumerate(STENCIL, 1):
        beside_all = (
            padded[:, 6 + offset : 6 + offset + planes]
            + padded[:, 6 - offset : 6 - offset + planes]
        )
        beside_all = beside_all + jnp.roll(field, offset, 2) + jnp.roll(field, -offset, 2)
        beside_all = beside_all + jnp.roll(field, offset, 3) + jnp.roll(field, -offset, 3)
        laplace = laplace + weight * beside_all
    return -0.5 * laplace + potential * field


def inner_rows(left, right):
    return lax.dot_general(
        left, right, (((1,), (1,)), ((), ())), preferred_element_type=jnp.float32
    )


def per_device(orbitals, potential, degrees):
    block_orbs = orbitals.shape[0]
    degree = degrees.reshape(1, 1, 1, 1)
    first = (hamiltonian(orbitals, potential) - SHIFT_C * orbitals) / HALF_W
    previous, current, picked = (orbitals, first, first)
    for order in range(2, DEG_MAX + 1):
        following = 2.0 * (hamiltonian(current, potential) - SHIFT_C * current) / HALF_W - previous
        picked = jnp.where(degree >= order, following, picked)
        previous, current = (current, following)
    filtered = picked.astype(jnp.bfloat16)
    cell_count = orbitals.shape[1] * orbitals.shape[2] * orbitals.shape[3]
    n_orb, n_dom = lax.axis_size("orb"), lax.axis_size("dom")
    total_cells = float(cell_count * n_dom)
    flattened = filtered.reshape(block_orbs, cell_count)
    mixed = lax.all_to_all(flattened, "orb", split_axis=1, concat_axis=0, tiled=True)
    partial_gram = inner_rows(mixed, mixed)
    rows = partial_gram.reshape(n_orb, 1, block_orbs, -1)
    sends = jnp.broadcast_to(rows, (n_orb, n_dom) + rows.shape[2:]).reshape((n_orb * n_dom,) + rows.shape[2:])
    gathered = lax.all_to_all(sends, ("orb", "dom"), split_axis=0, concat_axis=0, tiled=True)
    correlation = gathered.sum(axis=0) / total_cells
    return (filtered, correlation)


def solution(mesh):
    placed = (P("orb", "dom", None, None), P("dom", None, None), P("orb"))
    return jax.shard_map(
        per_device,
        mesh=mesh,
        in_specs=placed,
        out_specs=(P("orb", "dom", None, None), P("orb", None)),
        check_vma=False,
    )
```

```python
import functools

import jax
import jax.numpy as jnp
from jax import lax
from jax.experimental import pallas as pl
from jax.experimental.pallas import tpu as pltpu
from jax.sharding import PartitionSpec as P

DEG_MAX = 3


CENTER_COEF = -5369.0 / 1800.0
STENCIL = (12.0 / 7.0, -15.0 / 56.0, 10.0 / 189.0, -1.0 / 112.0, 2.0 / 1925.0, -1.0 / 16632.0)
SHIFT_C = 8.5
HALF_W = 4.5
RADIUS = len(STENCIL)


def shifted(x, k):
    count = lax.axis_size("dom")
    pairs = [(i, i + k) for i in range(count) if 0 <= i + k < count]
    if not pairs:
        return jnp.zeros_like(x)
    return lax.ppermute(x, "dom", pairs)


def wide_halo(orbitals, potential, orb_halo, pot_halo):
    slab = orbitals.shape[1]
    block_orbs = orbitals.shape[0]
    lefts, rights, pot_lefts, pot_rights = [], [], [], []
    k = 1
    while slab * (k - 1) < orb_halo:
        count = min(slab, orb_halo - slab * (k - 1))
        with_pot = slab * (k - 1) < pot_halo
        tail = orbitals[:, slab - count :]
        head = orbitals[:, :count]
        if with_pot:
            tail = jnp.concatenate([tail, potential[None, slab - count :]], axis=0)
            head = jnp.concatenate([head, potential[None, :count]], axis=0)
        got_left = shifted(tail, k)
        got_right = shifted(head, -k)
        lefts.insert(0, got_left[:block_orbs])
        rights.append(got_right[:block_orbs])
        if with_pot:
            pot_lefts.insert(0, got_left[block_orbs])
            pot_rights.append(got_right[block_orbs])
        else:
            pot_lefts.insert(0, jnp.zeros((count,) + potential.shape[1:], potential.dtype))
            pot_rights.append(jnp.zeros((count,) + potential.shape[1:], potential.dtype))
        k += 1
    cells = jnp.concatenate(lefts + [orbitals] + rights, axis=1)
    pot = jnp.concatenate(pot_lefts + [potential] + pot_rights, axis=0)
    return cells, pot


def filter_kernel(first_ref, deg_ref, cells_ref, pot_ref, out_ref, *iter_refs, grid_planes):
    block_orbs, _, ny, nz = cells_ref.shape
    slab = out_ref.shape[1]
    first = first_ref[0]
    degree = deg_ref[0]
    sources = (cells_ref,) + iter_refs

    def plane_value(order, b, p):
        source = sources[order - 1]
        field = source[b, RADIUS + p]
        laplace = (3.0 * CENTER_COEF) * field
        for offset, weight in enumerate(STENCIL, 1):
            beside_all = source[b, RADIUS + p + offset] + source[b, RADIUS + p - offset]
            beside_all = beside_all + pltpu.roll(field, offset, 0) + pltpu.roll(field, ny - offset, 0)
            beside_all = beside_all + pltpu.roll(field, offset, 1) + pltpu.roll(field, nz - offset, 1)
            laplace = laplace + weight * beside_all
        margin = (DEG_MAX - order) * RADIUS
        applied = -0.5 * laplace + pot_ref[order * RADIUS + p] * field
        if order == 1:
            return (applied - SHIFT_C * field) / HALF_W
        before = sources[order - 2][b, 2 * RADIUS + p]
        return 2.0 * (applied - SHIFT_C * field) / HALF_W - before

    for order in range(1, DEG_MAX):
        margin = (DEG_MAX - order) * RADIUS
        dest = iter_refs[order - 1]
        planes = slab + 2 * margin
        for b in range(block_orbs):
            def body(p, carry, order=order, b=b, dest=dest, margin=margin):
                value = plane_value(order, b, p)
                plane = first + order * RADIUS + p
                keep = jnp.full((ny, nz), plane, jnp.int32)
                keep = (keep >= 0) & (keep < grid_planes)
                dest[b, p] = jnp.where(keep, value, 0.0)
                return carry
            lax.fori_loop(0, planes, body, 0)

    for b in range(block_orbs):
        def last(p, carry, b=b):
            value = plane_value(DEG_MAX, b, p)
            levels = jnp.full((ny, nz), degree, jnp.int32)
            picked = iter_refs[0][b, (DEG_MAX - 1) * RADIUS + p]
            for order in range(2, DEG_MAX):
                picked = jnp.where(levels >= order, iter_refs[order - 1][b, (DEG_MAX - order) * RADIUS + p], picked)
            picked = jnp.where(levels >= DEG_MAX, value, picked)
            out_ref[b, p] = picked.astype(out_ref.dtype)
            return carry
        lax.fori_loop(0, slab, last, 0)


def chebyshev_filter(cells, pot, first, degree, grid_planes):
    block_orbs, planes, ny, nz = cells.shape
    slab = planes - 2 * DEG_MAX * RADIUS
    smem = pl.BlockSpec(memory_space=pltpu.SMEM)
    vmem = pl.BlockSpec(memory_space=pltpu.VMEM)
    return pl.pallas_call(
        functools.partial(filter_kernel, grid_planes=grid_planes),
        out_shape=jax.ShapeDtypeStruct((block_orbs, slab, ny, nz), jnp.bfloat16),
        in_specs=[smem, smem, vmem, vmem],
        out_specs=vmem,
        scratch_shapes=[
            pltpu.VMEM((block_orbs, slab + 2 * (DEG_MAX - order) * RADIUS, ny, nz), jnp.float32)
            for order in range(1, DEG_MAX)
        ],
    )(first, degree, cells, pot)


def inner_rows(left, right):
    return lax.dot_general(
        left, right, (((1,), (1,)), ((), ())), preferred_element_type=jnp.float32
    )


def per_device(orbitals, potential, degrees):
    block_orbs, slab = orbitals.shape[0], orbitals.shape[1]
    n_orb, n_dom = lax.axis_size("orb"), lax.axis_size("dom")
    grid_planes = slab * n_dom
    start = lax.axis_index("dom") * slab
    reach = DEG_MAX * RADIUS
    cells, pot = wide_halo(orbitals, potential, reach, reach - RADIUS)
    first = (start - reach).astype(jnp.int32).reshape(1)
    filtered = chebyshev_filter(cells, pot, first, degrees.astype(jnp.int32), grid_planes)
    cell_count = orbitals.shape[1] * orbitals.shape[2] * orbitals.shape[3]
    total_cells = float(cell_count * n_dom)
    flattened = filtered.reshape(block_orbs, cell_count)
    mixed = lax.all_to_all(flattened, "orb", split_axis=1, concat_axis=0, tiled=True)
    partial_gram = inner_rows(mixed, mixed)
    rows = partial_gram.reshape(n_orb, 1, block_orbs, -1)
    sends = jnp.broadcast_to(rows, (n_orb, n_dom) + rows.shape[2:]).reshape((n_orb * n_dom,) + rows.shape[2:])
    gathered = lax.all_to_all(sends, ("orb", "dom"), split_axis=0, concat_axis=0, tiled=True)
    correlation = gathered.sum(axis=0) / total_cells
    return (filtered, correlation)


def solution(mesh):
    placed = (P("orb", "dom", None, None), P("dom", None, None), P("orb"))
    return jax.shard_map(
        per_device,
        mesh=mesh,
        in_specs=placed,
        out_specs=(P("orb", "dom", None, None), P("orb", None)),
        check_vma=False,
    )
```

```python
import functools

import jax
import jax.numpy as jnp
from jax import lax
from jax.experimental import pallas as pl
from jax.experimental.pallas import tpu as pltpu
from jax.sharding import PartitionSpec as P

DEG_MAX = 3


CENTER_COEF = -5369.0 / 1800.0
STENCIL = (12.0 / 7.0, -15.0 / 56.0, 10.0 / 189.0, -1.0 / 112.0, 2.0 / 1925.0, -1.0 / 16632.0)
SHIFT_C = 8.5
HALF_W = 4.5
RADIUS = len(STENCIL)


def shifted(x, k):
    count = lax.axis_size("dom")
    pairs = [(i, i + k) for i in range(count) if 0 <= i + k < count]
    if not pairs:
        return jnp.zeros_like(x)
    return lax.ppermute(x, "dom", pairs)


def halo_pieces(values, axis, halo):
    slab = values.shape[axis]
    below, above = [], []
    k = 1
    while slab * (k - 1) < halo:
        count = min(slab, halo - slab * (k - 1))
        tail = lax.slice_in_dim(values, slab - count, slab, axis=axis)
        head = lax.slice_in_dim(values, 0, count, axis=axis)
        below.append(shifted(tail, k))
        above.append(shifted(head, -k))
        k += 1
    return below, above


def filter_kernel(first_ref, deg_ref, *refs, n_orb_pieces, n_pot_pieces, grid_planes):
    n_in = 2 + 2 * n_orb_pieces + 2 * n_pot_pieces
    ins = refs[:n_in]
    out_ref = refs[n_in]
    cells_ref, pot_ref, sems = refs[n_in + 1], refs[n_in + 2], refs[n_in + 3]
    iter_refs = refs[n_in + 4 :]
    orb_in, pot_in = ins[0], ins[1]
    orb_below = ins[2 : 2 + n_orb_pieces]
    orb_above = ins[2 + n_orb_pieces : 2 + 2 * n_orb_pieces]
    pot_below = ins[2 + 2 * n_orb_pieces : 2 + 2 * n_orb_pieces + n_pot_pieces]
    pot_above = ins[2 + 2 * n_orb_pieces + n_pot_pieces :]
    block_orbs, _, ny, nz = cells_ref.shape
    slab = out_ref.shape[1]
    first = first_ref[0]
    degree = deg_ref[0]

    copies = []

    def place(src, dst_ref, lo, axis):
        count = src.shape[axis]
        if axis == 1:
            dst = dst_ref.at[:, pl.ds(lo, count)]
        else:
            dst = dst_ref.at[pl.ds(lo, count)]
        copy = pltpu.make_async_copy(src, dst, sems.at[len(copies)])
        copy.start()
        copies.append(copy)

    reach = DEG_MAX * RADIUS
    place(orb_in, cells_ref, reach, 1)
    lo, hi = reach, reach + slab
    for piece_below, piece_above in zip(orb_below, orb_above):
        lo -= piece_below.shape[1]
        place(piece_below, cells_ref, lo, 1)
        place(piece_above, cells_ref, hi, 1)
        hi += piece_above.shape[1]
    pot_reach = reach - RADIUS
    place(pot_in, pot_ref, pot_reach, 0)
    lo, hi = pot_reach, pot_reach + slab
    for piece_below, piece_above in zip(pot_below, pot_above):
        lo -= piece_below.shape[0]
        place(piece_below, pot_ref, lo, 0)
        place(piece_above, pot_ref, hi, 0)
        hi += piece_above.shape[0]
    for copy in copies:
        copy.wait()

    sources = (cells_ref,) + tuple(iter_refs)

    def plane_value(order, b, p):
        source = sources[order - 1]
        field = source[b, RADIUS + p]
        laplace = (3.0 * CENTER_COEF) * field
        for offset, weight in enumerate(STENCIL, 1):
            beside_all = source[b, RADIUS + p + offset] + source[b, RADIUS + p - offset]
            beside_all = beside_all + pltpu.roll(field, offset, 0) + pltpu.roll(field, ny - offset, 0)
            beside_all = beside_all + pltpu.roll(field, offset, 1) + pltpu.roll(field, nz - offset, 1)
            laplace = laplace + weight * beside_all
        applied = -0.5 * laplace + pot_ref[(order - 1) * RADIUS + p] * field
        if order == 1:
            return (applied - SHIFT_C * field) / HALF_W
        before = sources[order - 2][b, 2 * RADIUS + p]
        return 2.0 * (applied - SHIFT_C * field) / HALF_W - before

    for order in range(1, DEG_MAX):
        margin = (DEG_MAX - order) * RADIUS
        dest = iter_refs[order - 1]
        planes = slab + 2 * margin
        for b in range(block_orbs):
            def body(p, carry, order=order, b=b, dest=dest):
                value = plane_value(order, b, p)
                plane = first + order * RADIUS + p
                keep = jnp.full((ny, nz), plane, jnp.int32)
                keep = (keep >= 0) & (keep < grid_planes)
                dest[b, p] = jnp.where(keep, value, 0.0)
                return carry
            lax.fori_loop(0, planes, body, 0)

    for b in range(block_orbs):
        def last(p, carry, b=b):
            value = plane_value(DEG_MAX, b, p)
            levels = jnp.full((ny, nz), degree, jnp.int32)
            picked = iter_refs[0][b, (DEG_MAX - 1) * RADIUS + p]
            for order in range(2, DEG_MAX):
                picked = jnp.where(levels >= order, iter_refs[order - 1][b, (DEG_MAX - order) * RADIUS + p], picked)
            picked = jnp.where(levels >= DEG_MAX, value, picked)
            out_ref[b, p] = picked.astype(out_ref.dtype)
            return carry
        lax.fori_loop(0, slab, last, 0)


def chebyshev_filter(orbitals, potential, first, degree, grid_planes):
    block_orbs, slab, ny, nz = orbitals.shape
    reach = DEG_MAX * RADIUS
    orb_below, orb_above = halo_pieces(orbitals, 1, reach)
    pot_below, pot_above = halo_pieces(potential, 0, reach - RADIUS)
    operands = [orbitals, potential] + orb_below + orb_above + pot_below + pot_above
    smem = pl.BlockSpec(memory_space=pltpu.SMEM)
    hbm = pl.BlockSpec(memory_space=pl.ANY)
    vmem = pl.BlockSpec(memory_space=pltpu.VMEM)
    n_copies = len(operands)
    return pl.pallas_call(
        functools.partial(
            filter_kernel,
            n_orb_pieces=len(orb_below),
            n_pot_pieces=len(pot_below),
            grid_planes=grid_planes,
        ),
        out_shape=jax.ShapeDtypeStruct((block_orbs, slab, ny, nz), jnp.bfloat16),
        in_specs=[smem, smem] + [hbm] * n_copies,
        out_specs=vmem,
        scratch_shapes=[
            pltpu.VMEM((block_orbs, slab + 2 * reach, ny, nz), jnp.float32),
            pltpu.VMEM((slab + 2 * (reach - RADIUS), ny, nz), jnp.float32),
            pltpu.SemaphoreType.DMA((n_copies,)),
        ]
        + [
            pltpu.VMEM((block_orbs, slab + 2 * (DEG_MAX - order) * RADIUS, ny, nz), jnp.float32)
            for order in range(1, DEG_MAX)
        ],
    )(first, degree, *operands)


def inner_rows(left, right):
    return lax.dot_general(
        left, right, (((1,), (1,)), ((), ())), preferred_element_type=jnp.float32
    )


def per_device(orbitals, potential, degrees):
    block_orbs, slab = orbitals.shape[0], orbitals.shape[1]
    n_orb, n_dom = lax.axis_size("orb"), lax.axis_size("dom")
    grid_planes = slab * n_dom
    start = lax.axis_index("dom") * slab
    first = (start - DEG_MAX * RADIUS).astype(jnp.int32).reshape(1)
    filtered = chebyshev_filter(orbitals, potential, first, degrees.astype(jnp.int32), grid_planes)
    cell_count = orbitals.shape[1] * orbitals.shape[2] * orbitals.shape[3]
    total_cells = float(cell_count * n_dom)
    flattened = filtered.reshape(block_orbs, cell_count)
    mixed = lax.all_to_all(flattened, "orb", split_axis=1, concat_axis=0, tiled=True)
    partial_gram = inner_rows(mixed, mixed)
    rows = partial_gram.reshape(n_orb, 1, block_orbs, -1)
    sends = jnp.broadcast_to(rows, (n_orb, n_dom) + rows.shape[2:]).reshape((n_orb * n_dom,) + rows.shape[2:])
    gathered = lax.all_to_all(sends, ("orb", "dom"), split_axis=0, concat_axis=0, tiled=True)
    correlation = gathered.sum(axis=0) / total_cells
    return (filtered, correlation)


def solution(mesh):
    placed = (P("orb", "dom", None, None), P("dom", None, None), P("orb"))
    return jax.shard_map(
        per_device,
        mesh=mesh,
        in_specs=placed,
        out_specs=(P("orb", "dom", None, None), P("orb", None)),
        check_vma=False,
    )
```

```python
import functools

import numpy as np
import jax
import jax.numpy as jnp
from jax import lax
from jax.experimental import pallas as pl
from jax.experimental.pallas import tpu as pltpu
from jax.sharding import PartitionSpec as P

DEG_MAX = 3


CENTER_COEF = -5369.0 / 1800.0
STENCIL = (12.0 / 7.0, -15.0 / 56.0, 10.0 / 189.0, -1.0 / 112.0, 2.0 / 1925.0, -1.0 / 16632.0)
SHIFT_C = 8.5
HALF_W = 4.5
RADIUS = len(STENCIL)


def circulant(n):
    gap = (np.arange(n)[None, :] - np.arange(n)[:, None]) % n
    weights = np.zeros((n, n), np.float32)
    for offset, weight in enumerate(STENCIL, 1):
        weights[(gap == offset) | (gap == n - offset)] = np.float32(weight)
    return weights


def shifted(x, k):
    count = lax.axis_size("dom")
    pairs = [(i, i + k) for i in range(count) if 0 <= i + k < count]
    if not pairs:
        return jnp.zeros_like(x)
    return lax.ppermute(x, "dom", pairs)


def halo_pieces(values, axis, halo):
    slab = values.shape[axis]
    below, above = [], []
    k = 1
    while slab * (k - 1) < halo:
        count = min(slab, halo - slab * (k - 1))
        tail = lax.slice_in_dim(values, slab - count, slab, axis=axis)
        head = lax.slice_in_dim(values, 0, count, axis=axis)
        below.append(shifted(tail, k))
        above.append(shifted(head, -k))
        k += 1
    return below, above


def filter_kernel(first_ref, deg_ref, cz_ref, *refs, n_orb_pieces, n_pot_pieces, grid_planes):
    n_in = 2 + 2 * n_orb_pieces + 2 * n_pot_pieces
    ins = refs[:n_in]
    out_ref = refs[n_in]
    cells_ref, pot_ref, zsum_ref, sems = refs[n_in + 1 : n_in + 5]
    iter_refs = refs[n_in + 5 :]
    orb_in, pot_in = ins[0], ins[1]
    orb_below = ins[2 : 2 + n_orb_pieces]
    orb_above = ins[2 + n_orb_pieces : 2 + 2 * n_orb_pieces]
    pot_below = ins[2 + 2 * n_orb_pieces : 2 + 2 * n_orb_pieces + n_pot_pieces]
    pot_above = ins[2 + 2 * n_orb_pieces + n_pot_pieces :]
    block_orbs, _, ny, nz = cells_ref.shape
    slab = out_ref.shape[1]
    first = first_ref[0]
    degree = deg_ref[0]

    copies = []

    def place(src, dst_ref, lo, axis):
        count = src.shape[axis]
        if axis == 1:
            dst = dst_ref.at[:, pl.ds(lo, count)]
        else:
            dst = dst_ref.at[pl.ds(lo, count)]
        copy = pltpu.make_async_copy(src, dst, sems.at[len(copies)])
        copy.start()
        copies.append(copy)

    reach = DEG_MAX * RADIUS
    place(orb_in, cells_ref, reach, 1)
    lo, hi = reach, reach + slab
    for piece_below, piece_above in zip(orb_below, orb_above):
        lo -= piece_below.shape[1]
        place(piece_below, cells_ref, lo, 1)
        place(piece_above, cells_ref, hi, 1)
        hi += piece_above.shape[1]
    pot_reach = reach - RADIUS
    place(pot_in, pot_ref, pot_reach, 0)
    lo, hi = pot_reach, pot_reach + slab
    for piece_below, piece_above in zip(pot_below, pot_above):
        lo -= piece_below.shape[0]
        place(piece_below, pot_ref, lo, 0)
        place(piece_above, pot_ref, hi, 0)
        hi += piece_above.shape[0]
    for copy in copies:
        copy.wait()

    sources = (cells_ref,) + tuple(iter_refs)

    def plane_value(order, b, p):
        source = sources[order - 1]
        field = source[b, RADIUS + p]
        laplace = (3.0 * CENTER_COEF) * field
        for offset, weight in enumerate(STENCIL, 1):
            beside_all = source[b, RADIUS + p + offset] + source[b, RADIUS + p - offset]
            beside_all = beside_all + pltpu.roll(field, offset, 0) + pltpu.roll(field, ny - offset, 0)
            laplace = laplace + weight * beside_all
        laplace = laplace + zsum_ref[b, p]
        applied = -0.5 * laplace + pot_ref[(order - 1) * RADIUS + p] * field
        if order == 1:
            return (applied - SHIFT_C * field) / HALF_W
        before = sources[order - 2][b, 2 * RADIUS + p]
        return 2.0 * (applied - SHIFT_C * field) / HALF_W - before

    def along_z(order, planes):
        source = sources[order - 1]
        for b in range(block_orbs):
            rows = source[b, RADIUS : RADIUS + planes].reshape(planes * ny, nz)
            mixed = jnp.dot(rows, cz_ref[...], precision=lax.Precision.HIGHEST, preferred_element_type=jnp.float32)
            zsum_ref[b, :planes] = mixed.reshape(planes, ny, nz)

    for order in range(1, DEG_MAX):
        margin = (DEG_MAX - order) * RADIUS
        dest = iter_refs[order - 1]
        planes = slab + 2 * margin
        along_z(order, planes)
        for b in range(block_orbs):
            def body(p, carry, order=order, b=b, dest=dest):
                value = plane_value(order, b, p)
                plane = first + order * RADIUS + p
                keep = jnp.full((ny, nz), plane, jnp.int32)
                keep = (keep >= 0) & (keep < grid_planes)
                dest[b, p] = jnp.where(keep, value, 0.0)
                return carry
            lax.fori_loop(0, planes, body, 0, unroll=2)

    along_z(DEG_MAX, slab)
    for b in range(block_orbs):
        def last(p, carry, b=b):
            value = plane_value(DEG_MAX, b, p)
            levels = jnp.full((ny, nz), degree, jnp.int32)
            picked = iter_refs[0][b, (DEG_MAX - 1) * RADIUS + p]
            for order in range(2, DEG_MAX):
                picked = jnp.where(levels >= order, iter_refs[order - 1][b, (DEG_MAX - order) * RADIUS + p], picked)
            picked = jnp.where(levels >= DEG_MAX, value, picked)
            out_ref[b, p] = picked.astype(out_ref.dtype)
            return carry
        lax.fori_loop(0, slab, last, 0, unroll=2)


def chebyshev_filter(orbitals, potential, first, degree, grid_planes):
    block_orbs, slab, ny, nz = orbitals.shape
    reach = DEG_MAX * RADIUS
    orb_below, orb_above = halo_pieces(orbitals, 1, reach)
    pot_below, pot_above = halo_pieces(potential, 0, reach - RADIUS)
    operands = [orbitals, potential] + orb_below + orb_above + pot_below + pot_above
    smem = pl.BlockSpec(memory_space=pltpu.SMEM)
    hbm = pl.BlockSpec(memory_space=pl.ANY)
    vmem = pl.BlockSpec(memory_space=pltpu.VMEM)
    n_copies = len(operands)
    return pl.pallas_call(
        functools.partial(
            filter_kernel,
            n_orb_pieces=len(orb_below),
            n_pot_pieces=len(pot_below),
            grid_planes=grid_planes,
        ),
        out_shape=jax.ShapeDtypeStruct((block_orbs, slab, ny, nz), jnp.bfloat16),
        in_specs=[smem, smem, vmem] + [hbm] * n_copies,
        out_specs=vmem,
        scratch_shapes=[
            pltpu.VMEM((block_orbs, slab + 2 * reach, ny, nz), jnp.float32),
            pltpu.VMEM((slab + 2 * (reach - RADIUS), ny, nz), jnp.float32),
            pltpu.VMEM((block_orbs, slab + 2 * (reach - RADIUS), ny, nz), jnp.float32),
            pltpu.SemaphoreType.DMA((n_copies,)),
        ]
        + [
            pltpu.VMEM((block_orbs, slab + 2 * (DEG_MAX - order) * RADIUS, ny, nz), jnp.float32)
            for order in range(1, DEG_MAX)
        ],
    )(first, degree, jnp.asarray(circulant(nz)), *operands)


def inner_rows(left, right):
    return lax.dot_general(
        left, right, (((1,), (1,)), ((), ())), preferred_element_type=jnp.float32
    )


def per_device(orbitals, potential, degrees):
    block_orbs, slab = orbitals.shape[0], orbitals.shape[1]
    n_orb, n_dom = lax.axis_size("orb"), lax.axis_size("dom")
    grid_planes = slab * n_dom
    start = lax.axis_index("dom") * slab
    first = (start - DEG_MAX * RADIUS).astype(jnp.int32).reshape(1)
    filtered = chebyshev_filter(orbitals, potential, first, degrees.astype(jnp.int32), grid_planes)
    cell_count = orbitals.shape[1] * orbitals.shape[2] * orbitals.shape[3]
    total_cells = float(cell_count * n_dom)
    flattened = filtered.reshape(block_orbs, cell_count)
    mixed = lax.all_to_all(flattened, "orb", split_axis=1, concat_axis=0, tiled=True)
    partial_gram = inner_rows(mixed, mixed)
    rows = partial_gram.reshape(n_orb, 1, block_orbs, -1)
    sends = jnp.broadcast_to(rows, (n_orb, n_dom) + rows.shape[2:]).reshape((n_orb * n_dom,) + rows.shape[2:])
    gathered = lax.all_to_all(sends, ("orb", "dom"), split_axis=0, concat_axis=0, tiled=True)
    correlation = gathered.sum(axis=0) / total_cells
    return (filtered, correlation)


def solution(mesh):
    placed = (P("orb", "dom", None, None), P("dom", None, None), P("orb"))
    return jax.shard_map(
        per_device,
        mesh=mesh,
        in_specs=placed,
        out_specs=(P("orb", "dom", None, None), P("orb", None)),
        check_vma=False,
    )
```

```python
import functools

import numpy as np
import jax
import jax.numpy as jnp
from jax import lax
from jax.experimental import pallas as pl
from jax.experimental.pallas import tpu as pltpu
from jax.sharding import PartitionSpec as P

DEG_MAX = 3


CENTER_COEF = -5369.0 / 1800.0
STENCIL = (12.0 / 7.0, -15.0 / 56.0, 10.0 / 189.0, -1.0 / 112.0, 2.0 / 1925.0, -1.0 / 16632.0)
SHIFT_C = 8.5
HALF_W = 4.5
RADIUS = len(STENCIL)


def circulant(n):
    gap = (np.arange(n)[None, :] - np.arange(n)[:, None]) % n
    weights = np.zeros((n, n), np.float32)
    for offset, weight in enumerate(STENCIL, 1):
        weights[(gap == offset) | (gap == n - offset)] = np.float32(weight)
    return weights


def shifted(x, k):
    count = lax.axis_size("dom")
    pairs = [(i, i + k) for i in range(count) if 0 <= i + k < count]
    if not pairs:
        return jnp.zeros_like(x)
    return lax.ppermute(x, "dom", pairs)


def halo_plan(orbitals, potential, reach, pot_reach):
    block_orbs, slab = orbitals.shape[0], orbitals.shape[1]
    operands = [orbitals, potential]
    copies = [(0, "all", "cells", reach), (1, "all", "pot", pot_reach)]
    packed = None
    k = 1
    while slab * (k - 1) < reach:
        count = min(slab, reach - slab * (k - 1))
        pot_count = max(0, min(slab, pot_reach - slab * (k - 1)))
        for sign in (1, -1):
            if pot_count == slab and count == slab:
                if packed is None:
                    packed = jnp.concatenate([orbitals, potential[None]], axis=0)
                parts = [(packed, "orb", count, "cells", reach), (None, "pot", count, "pot", pot_reach)]
            else:
                parts = [(orbitals, "all", count, "cells", reach)]
                if pot_count:
                    parts.append((potential, "all", pot_count, "pot", pot_reach))
            for values, part, size, dest, centre in parts:
                lo = centre - slab * (k - 1) - size if sign > 0 else centre + slab * k
                if values is not None:
                    axis = 0 if values is potential else 1
                    span = values.shape[axis]
                    if sign > 0:
                        piece = lax.slice_in_dim(values, span - size, span, axis=axis)
                    else:
                        piece = lax.slice_in_dim(values, 0, size, axis=axis)
                    operands.append(shifted(piece, sign * k))
                copies.append((len(operands) - 1, part, dest, lo))
        k += 1
    return operands, copies


def filter_kernel(first_ref, deg_ref, cz_ref, *refs, copies, n_in, block_count, grid_planes):
    ins = refs[:n_in]
    out_ref = refs[n_in]
    cells_ref, pot_ref, zsum_ref, sems = refs[n_in + 1 : n_in + 5]
    iter_refs = refs[n_in + 5 :]
    block_orbs, _, ny, nz = cells_ref.shape
    slab = out_ref.shape[1]
    first = first_ref[0]
    degree = deg_ref[0]

    started = []
    for index, part, dest, lo in copies:
        source = ins[index]
        if part == "orb":
            source = source.at[pl.ds(0, block_count)]
        elif part == "pot":
            source = source.at[block_count]
        if dest == "cells":
            target = cells_ref.at[:, pl.ds(lo, source.shape[1])]
        else:
            target = pot_ref.at[pl.ds(lo, source.shape[0])]
        copy = pltpu.make_async_copy(source, target, sems.at[len(started)])
        copy.start()
        started.append(copy)
    for copy in started:
        copy.wait()

    sources = (cells_ref,) + tuple(iter_refs)

    def plane_value(order, b, p):
        source = sources[order - 1]
        field = source[b, RADIUS + p]
        laplace = (3.0 * CENTER_COEF) * field
        for offset, weight in enumerate(STENCIL, 1):
            beside_all = source[b, RADIUS + p + offset] + source[b, RADIUS + p - offset]
            beside_all = beside_all + pltpu.roll(field, offset, 0) + pltpu.roll(field, ny - offset, 0)
            laplace = laplace + weight * beside_all
        laplace = laplace + zsum_ref[b, p]
        applied = -0.5 * laplace + pot_ref[(order - 1) * RADIUS + p] * field
        if order == 1:
            return (applied - SHIFT_C * field) / HALF_W
        before = sources[order - 2][b, 2 * RADIUS + p]
        return 2.0 * (applied - SHIFT_C * field) / HALF_W - before

    def along_z(order, planes):
        source = sources[order - 1]
        for b in range(block_orbs):
            rows = source[b, RADIUS : RADIUS + planes].reshape(planes * ny, nz)
            mixed = jnp.dot(rows, cz_ref[...], precision=lax.Precision.HIGHEST, preferred_element_type=jnp.float32)
            zsum_ref[b, :planes] = mixed.reshape(planes, ny, nz)

    for order in range(1, DEG_MAX):
        margin = (DEG_MAX - order) * RADIUS
        dest = iter_refs[order - 1]
        planes = slab + 2 * margin
        along_z(order, planes)
        for b in range(block_orbs):
            def body(p, carry, order=order, b=b, dest=dest):
                value = plane_value(order, b, p)
                plane = first + order * RADIUS + p
                keep = jnp.full((ny, nz), plane, jnp.int32)
                keep = (keep >= 0) & (keep < grid_planes)
                dest[b, p] = jnp.where(keep, value, 0.0)
                return carry
            lax.fori_loop(0, planes, body, 0, unroll=2)

    along_z(DEG_MAX, slab)
    for b in range(block_orbs):
        def last(p, carry, b=b):
            value = plane_value(DEG_MAX, b, p)
            levels = jnp.full((ny, nz), degree, jnp.int32)
            picked = iter_refs[0][b, (DEG_MAX - 1) * RADIUS + p]
            for order in range(2, DEG_MAX):
                picked = jnp.where(levels >= order, iter_refs[order - 1][b, (DEG_MAX - order) * RADIUS + p], picked)
            picked = jnp.where(levels >= DEG_MAX, value, picked)
            out_ref[b, p] = picked.astype(out_ref.dtype)
            return carry
        lax.fori_loop(0, slab, last, 0, unroll=2)


def chebyshev_filter(orbitals, potential, first, degree, grid_planes):
    block_orbs, slab, ny, nz = orbitals.shape
    reach = DEG_MAX * RADIUS
    operands, copies = halo_plan(orbitals, potential, reach, reach - RADIUS)
    smem = pl.BlockSpec(memory_space=pltpu.SMEM)
    hbm = pl.BlockSpec(memory_space=pl.ANY)
    vmem = pl.BlockSpec(memory_space=pltpu.VMEM)
    return pl.pallas_call(
        functools.partial(
            filter_kernel,
            copies=tuple(copies),
            n_in=len(operands),
            block_count=block_orbs,
            grid_planes=grid_planes,
        ),
        out_shape=jax.ShapeDtypeStruct((block_orbs, slab, ny, nz), jnp.bfloat16),
        in_specs=[smem, smem, vmem] + [hbm] * len(operands),
        out_specs=vmem,
        scratch_shapes=[
            pltpu.VMEM((block_orbs, slab + 2 * reach, ny, nz), jnp.float32),
            pltpu.VMEM((slab + 2 * (reach - RADIUS), ny, nz), jnp.float32),
            pltpu.VMEM((block_orbs, slab + 2 * (reach - RADIUS), ny, nz), jnp.float32),
            pltpu.SemaphoreType.DMA((len(copies),)),
        ]
        + [
            pltpu.VMEM((block_orbs, slab + 2 * (DEG_MAX - order) * RADIUS, ny, nz), jnp.float32)
            for order in range(1, DEG_MAX)
        ],
    )(first, degree, jnp.asarray(circulant(nz)), *operands)


def inner_rows(left, right):
    return lax.dot_general(
        left, right, (((1,), (1,)), ((), ())), preferred_element_type=jnp.float32
    )


def per_device(orbitals, potential, degrees):
    block_orbs, slab = orbitals.shape[0], orbitals.shape[1]
    n_orb, n_dom = lax.axis_size("orb"), lax.axis_size("dom")
    grid_planes = slab * n_dom
    start = lax.axis_index("dom") * slab
    first = (start - DEG_MAX * RADIUS).astype(jnp.int32).reshape(1)
    filtered = chebyshev_filter(orbitals, potential, first, degrees.astype(jnp.int32), grid_planes)
    cell_count = orbitals.shape[1] * orbitals.shape[2] * orbitals.shape[3]
    total_cells = float(cell_count * n_dom)
    flattened = filtered.reshape(block_orbs, cell_count)
    mixed = lax.all_to_all(flattened, "orb", split_axis=1, concat_axis=0, tiled=True)
    partial_gram = inner_rows(mixed, mixed)
    rows = partial_gram.reshape(n_orb, 1, block_orbs, -1)
    sends = jnp.broadcast_to(rows, (n_orb, n_dom) + rows.shape[2:]).reshape((n_orb * n_dom,) + rows.shape[2:])
    gathered = lax.all_to_all(sends, ("orb", "dom"), split_axis=0, concat_axis=0, tiled=True)
    correlation = gathered.sum(axis=0) / total_cells
    return (filtered, correlation)


def solution(mesh):
    placed = (P("orb", "dom", None, None), P("dom", None, None), P("orb"))
    return jax.shard_map(
        per_device,
        mesh=mesh,
        in_specs=placed,
        out_specs=(P("orb", "dom", None, None), P("orb", None)),
        check_vma=False,
    )
```

```python
import functools

import numpy as np
import jax
import jax.numpy as jnp
from jax import lax
from jax.experimental import pallas as pl
from jax.experimental.pallas import tpu as pltpu
from jax.sharding import PartitionSpec as P

DEG_MAX = 3


CENTER_COEF = -5369.0 / 1800.0
STENCIL = (12.0 / 7.0, -15.0 / 56.0, 10.0 / 189.0, -1.0 / 112.0, 2.0 / 1925.0, -1.0 / 16632.0)
SHIFT_C = 8.5
HALF_W = 4.5
RADIUS = len(STENCIL)


def circulant(n):
    gap = (np.arange(n)[None, :] - np.arange(n)[:, None]) % n
    weights = np.zeros((n, n), np.float32)
    for offset, weight in enumerate(STENCIL, 1):
        weights[(gap == offset) | (gap == n - offset)] = np.float32(weight)
    return weights


def shifted(x, k):
    count = lax.axis_size("dom")
    pairs = [(i, i + k) for i in range(count) if 0 <= i + k < count]
    if not pairs:
        return jnp.zeros_like(x)
    return lax.ppermute(x, "dom", pairs)


def gather_plan(orbitals, potential, reach, pot_reach):
    block_orbs, slab = orbitals.shape[0], orbitals.shape[1]
    count = lax.axis_size("dom")
    packed = jnp.concatenate([orbitals, potential[None]], axis=0)
    operands = [orbitals, potential]
    copies = [(0, "all", "cells", reach, None), (1, "all", "pot", pot_reach, None)]
    zeros = []
    for k in range(1, count):
        operands.append(lax.ppermute(packed, "dom", [(i, (i + k) % count) for i in range(count)]))
    for rel in range(-(reach // slab), reach // slab + 1):
        if rel == 0:
            continue
        piece = 1 + (-rel) % count
        copies.append((piece, "orb", "cells", reach + rel * slab, rel))
        zeros.append(("cells", reach + rel * slab, rel))
        if abs(rel) * slab <= pot_reach:
            copies.append((piece, "pot", "pot", pot_reach + rel * slab, rel))
            zeros.append(("pot", pot_reach + rel * slab, rel))
    return operands, copies, zeros


def halo_plan(orbitals, potential, reach, pot_reach):
    block_orbs, slab = orbitals.shape[0], orbitals.shape[1]
    if reach % slab == 0 and pot_reach % slab == 0 and lax.axis_size("dom") - 1 <= reach // slab:
        return gather_plan(orbitals, potential, reach, pot_reach)
    operands = [orbitals, potential]
    copies = [(0, "all", "cells", reach, None), (1, "all", "pot", pot_reach, None)]
    packed = None
    k = 1
    while slab * (k - 1) < reach:
        count = min(slab, reach - slab * (k - 1))
        pot_count = max(0, min(slab, pot_reach - slab * (k - 1)))
        for sign in (1, -1):
            if pot_count == slab and count == slab:
                if packed is None:
                    packed = jnp.concatenate([orbitals, potential[None]], axis=0)
                parts = [(packed, "orb", count, "cells", reach), (None, "pot", count, "pot", pot_reach)]
            else:
                parts = [(orbitals, "all", count, "cells", reach)]
                if pot_count:
                    parts.append((potential, "all", pot_count, "pot", pot_reach))
            for values, part, size, dest, centre in parts:
                lo = centre - slab * (k - 1) - size if sign > 0 else centre + slab * k
                if values is not None:
                    axis = 0 if values is potential else 1
                    span = values.shape[axis]
                    if sign > 0:
                        piece = lax.slice_in_dim(values, span - size, span, axis=axis)
                    else:
                        piece = lax.slice_in_dim(values, 0, size, axis=axis)
                    operands.append(shifted(piece, sign * k))
                copies.append((len(operands) - 1, part, dest, lo, None))
        k += 1
    return operands, copies, []


def filter_kernel(first_ref, deg_ref, cz_ref, *refs, copies, zeros, n_in, block_count, grid_planes):
    ins = refs[:n_in]
    out_ref = refs[n_in]
    cells_ref, pot_ref, zsum_ref, sems = refs[n_in + 1 : n_in + 5]
    iter_refs = refs[n_in + 5 :]
    block_orbs, _, ny, nz = cells_ref.shape
    slab = out_ref.shape[1]
    first = first_ref[0]
    degree = deg_ref[0]

    reach = DEG_MAX * RADIUS
    own_slab = (first + reach) // slab

    def inside(rel):
        return (own_slab + rel >= 0) & (own_slab + rel < grid_planes // slab)

    for dest, lo, rel in zeros:
        def clear(dest=dest, lo=lo):
            if dest == "cells":
                cells_ref[:, pl.ds(lo, slab)] = jnp.zeros((block_orbs, slab, ny, nz), jnp.float32)
            else:
                pot_ref[pl.ds(lo, slab)] = jnp.zeros((slab, ny, nz), jnp.float32)
        pl.when(jnp.logical_not(inside(rel)))(clear)
    started = []
    for index, part, dest, lo, rel in copies:
        source = ins[index]
        if part == "orb":
            source = source.at[pl.ds(0, block_count)]
        elif part == "pot":
            source = source.at[block_count]
        if dest == "cells":
            target = cells_ref.at[:, pl.ds(lo, source.shape[1])]
        else:
            target = pot_ref.at[pl.ds(lo, source.shape[0])]
        copy = pltpu.make_async_copy(source, target, sems.at[len(started)])
        if rel is None:
            copy.start()
        else:
            pl.when(inside(rel))(copy.start)
        started.append((copy, rel))
    for copy, rel in started:
        if rel is None:
            copy.wait()
        else:
            pl.when(inside(rel))(copy.wait)

    sources = (cells_ref,) + tuple(iter_refs)

    def plane_value(order, b, p):
        source = sources[order - 1]
        field = source[b, RADIUS + p]
        laplace = (3.0 * CENTER_COEF) * field
        for offset, weight in enumerate(STENCIL, 1):
            beside_all = source[b, RADIUS + p + offset] + source[b, RADIUS + p - offset]
            beside_all = beside_all + pltpu.roll(field, offset, 0) + pltpu.roll(field, ny - offset, 0)
            laplace = laplace + weight * beside_all
        laplace = laplace + zsum_ref[b, p]
        applied = -0.5 * laplace + pot_ref[(order - 1) * RADIUS + p] * field
        if order == 1:
            return (applied - SHIFT_C * field) / HALF_W
        before = sources[order - 2][b, 2 * RADIUS + p]
        return 2.0 * (applied - SHIFT_C * field) / HALF_W - before

    def along_z(order, planes):
        source = sources[order - 1]
        for b in range(block_orbs):
            rows = source[b, RADIUS : RADIUS + planes].reshape(planes * ny, nz)
            mixed = jnp.dot(rows, cz_ref[...], precision=lax.Precision.HIGHEST, preferred_element_type=jnp.float32)
            zsum_ref[b, :planes] = mixed.reshape(planes, ny, nz)

    for order in range(1, DEG_MAX):
        margin = (DEG_MAX - order) * RADIUS
        dest = iter_refs[order - 1]
        planes = slab + 2 * margin
        along_z(order, planes)
        for b in range(block_orbs):
            def body(p, carry, order=order, b=b, dest=dest):
                value = plane_value(order, b, p)
                plane = first + order * RADIUS + p
                keep = jnp.full((ny, nz), plane, jnp.int32)
                keep = (keep >= 0) & (keep < grid_planes)
                dest[b, p] = jnp.where(keep, value, 0.0)
                return carry
            lax.fori_loop(0, planes, body, 0, unroll=2)

    along_z(DEG_MAX, slab)
    for b in range(block_orbs):
        def last(p, carry, b=b):
            value = plane_value(DEG_MAX, b, p)
            levels = jnp.full((ny, nz), degree, jnp.int32)
            picked = iter_refs[0][b, (DEG_MAX - 1) * RADIUS + p]
            for order in range(2, DEG_MAX):
                picked = jnp.where(levels >= order, iter_refs[order - 1][b, (DEG_MAX - order) * RADIUS + p], picked)
            picked = jnp.where(levels >= DEG_MAX, value, picked)
            out_ref[b, p] = picked.astype(out_ref.dtype)
            return carry
        lax.fori_loop(0, slab, last, 0, unroll=2)


def chebyshev_filter(orbitals, potential, first, degree, grid_planes):
    block_orbs, slab, ny, nz = orbitals.shape
    reach = DEG_MAX * RADIUS
    operands, copies, zeros = halo_plan(orbitals, potential, reach, reach - RADIUS)
    smem = pl.BlockSpec(memory_space=pltpu.SMEM)
    hbm = pl.BlockSpec(memory_space=pl.ANY)
    vmem = pl.BlockSpec(memory_space=pltpu.VMEM)
    return pl.pallas_call(
        functools.partial(
            filter_kernel,
            copies=tuple(copies),
            zeros=tuple(zeros),
            n_in=len(operands),
            block_count=block_orbs,
            grid_planes=grid_planes,
        ),
        out_shape=jax.ShapeDtypeStruct((block_orbs, slab, ny, nz), jnp.bfloat16),
        in_specs=[smem, smem, vmem] + [hbm] * len(operands),
        out_specs=vmem,
        scratch_shapes=[
            pltpu.VMEM((block_orbs, slab + 2 * reach, ny, nz), jnp.float32),
            pltpu.VMEM((slab + 2 * (reach - RADIUS), ny, nz), jnp.float32),
            pltpu.VMEM((block_orbs, slab + 2 * (reach - RADIUS), ny, nz), jnp.float32),
            pltpu.SemaphoreType.DMA((len(copies),)),
        ]
        + [
            pltpu.VMEM((block_orbs, slab + 2 * (DEG_MAX - order) * RADIUS, ny, nz), jnp.float32)
            for order in range(1, DEG_MAX)
        ],
    )(first, degree, jnp.asarray(circulant(nz)), *operands)


def inner_rows(left, right):
    return lax.dot_general(
        left, right, (((1,), (1,)), ((), ())), preferred_element_type=jnp.float32
    )


def per_device(orbitals, potential, degrees):
    block_orbs, slab = orbitals.shape[0], orbitals.shape[1]
    n_orb, n_dom = lax.axis_size("orb"), lax.axis_size("dom")
    grid_planes = slab * n_dom
    start = lax.axis_index("dom") * slab
    first = (start - DEG_MAX * RADIUS).astype(jnp.int32).reshape(1)
    filtered = chebyshev_filter(orbitals, potential, first, degrees.astype(jnp.int32), grid_planes)
    cell_count = orbitals.shape[1] * orbitals.shape[2] * orbitals.shape[3]
    total_cells = float(cell_count * n_dom)
    flattened = filtered.reshape(block_orbs, cell_count)
    mixed = lax.all_to_all(flattened, "orb", split_axis=1, concat_axis=0, tiled=True)
    partial_gram = inner_rows(mixed, mixed)
    rows = partial_gram.reshape(n_orb, 1, block_orbs, -1)
    sends = jnp.broadcast_to(rows, (n_orb, n_dom) + rows.shape[2:]).reshape((n_orb * n_dom,) + rows.shape[2:])
    gathered = lax.all_to_all(sends, ("orb", "dom"), split_axis=0, concat_axis=0, tiled=True)
    correlation = gathered.sum(axis=0) / total_cells
    return (filtered, correlation)


def solution(mesh):
    placed = (P("orb", "dom", None, None), P("dom", None, None), P("orb"))
    return jax.shard_map(
        per_device,
        mesh=mesh,
        in_specs=placed,
        out_specs=(P("orb", "dom", None, None), P("orb", None)),
        check_vma=False,
    )
```

```python
import functools

import numpy as np
import jax
import jax.numpy as jnp
from jax import lax
from jax.experimental import pallas as pl
from jax.experimental.pallas import tpu as pltpu
from jax.sharding import PartitionSpec as P

DEG_MAX = 3


CENTER_COEF = -5369.0 / 1800.0
STENCIL = (12.0 / 7.0, -15.0 / 56.0, 10.0 / 189.0, -1.0 / 112.0, 2.0 / 1925.0, -1.0 / 16632.0)
SHIFT_C = 8.5
HALF_W = 4.5
RADIUS = len(STENCIL)


def circulant(n):
    gap = (np.arange(n)[None, :] - np.arange(n)[:, None]) % n
    weights = np.zeros((n, n), np.float32)
    for offset, weight in enumerate(STENCIL, 1):
        weights[(gap == offset) | (gap == n - offset)] = np.float32(weight)
    return weights


def shifted(x, k):
    count = lax.axis_size("dom")
    pairs = [(i, i + k) for i in range(count) if 0 <= i + k < count]
    if not pairs:
        return jnp.zeros_like(x)
    return lax.ppermute(x, "dom", pairs)


def cyclic_gather(send):
    count = lax.axis_size("dom")
    return [lax.ppermute(send, "dom", [(i, (i + k) % count) for i in range(count)]) for k in range(1, count)]


def gather_copies(first_piece, pot_first_piece, pot_row, reach, pot_reach, slab):
    count = lax.axis_size("dom")
    copies, zeros = [], []
    for rel in range(-(reach // slab), reach // slab + 1):
        if rel == 0:
            continue
        k = (-rel) % count
        if k == 0:
            zeros.append(("cells", reach + rel * slab, None))
        else:
            copies.append((first_piece + k - 1, (0, 1), "cells", reach + rel * slab, rel))
            zeros.append(("cells", reach + rel * slab, rel))
        if abs(rel) * slab <= pot_reach:
            if k == 0:
                zeros.append(("pot", pot_reach + rel * slab, None))
            else:
                copies.append((pot_first_piece + k - 1, pot_row, "pot", pot_reach + rel * slab, rel))
                zeros.append(("pot", pot_reach + rel * slab, rel))
    return copies, zeros


def halo_plan(orbitals, potential, reach, pot_reach):
    block_orbs, slab = orbitals.shape[0], orbitals.shape[1]
    operands = [orbitals, potential]
    copies = [(0, "all", "cells", reach, None), (1, "all", "pot", pot_reach, None)]
    packed = None
    k = 1
    while slab * (k - 1) < reach:
        count = min(slab, reach - slab * (k - 1))
        pot_count = max(0, min(slab, pot_reach - slab * (k - 1)))
        for sign in (1, -1):
            if pot_count == slab and count == slab:
                if packed is None:
                    packed = jnp.concatenate([orbitals, potential[None]], axis=0)
                parts = [(packed, "orb", count, "cells", reach), (None, "pot", count, "pot", pot_reach)]
            else:
                parts = [(orbitals, "all", count, "cells", reach)]
                if pot_count:
                    parts.append((potential, "all", pot_count, "pot", pot_reach))
            for values, part, size, dest, centre in parts:
                lo = centre - slab * (k - 1) - size if sign > 0 else centre + slab * k
                if values is not None:
                    axis = 0 if values is potential else 1
                    span = values.shape[axis]
                    if sign > 0:
                        piece = lax.slice_in_dim(values, span - size, span, axis=axis)
                    else:
                        piece = lax.slice_in_dim(values, 0, size, axis=axis)
                    operands.append(shifted(piece, sign * k))
                copies.append((len(operands) - 1, part, dest, lo, None))
        k += 1
    return operands, copies, []


def filter_kernel(first_ref, deg_ref, cz_ref, *refs, copies, zeros, n_in, block_count, grid_planes):
    ins = refs[:n_in]
    out_ref = refs[n_in]
    cells_ref, pot_ref, zsum_ref, sems = refs[n_in + 1 : n_in + 5]
    iter_refs = refs[n_in + 5 :]
    block_orbs, _, ny, nz = cells_ref.shape
    slab = out_ref.shape[1]
    first = first_ref[0]
    degree = deg_ref[0]

    reach = DEG_MAX * RADIUS
    own_slab = (first + reach) // slab

    def inside(rel):
        return (own_slab + rel >= 0) & (own_slab + rel < grid_planes // slab)

    for dest, lo, rel in zeros:
        def clear(dest=dest, lo=lo):
            if dest == "cells":
                cells_ref[:, pl.ds(lo, slab)] = jnp.zeros((block_orbs, slab, ny, nz), jnp.float32)
            else:
                pot_ref[pl.ds(lo, slab)] = jnp.zeros((slab, ny, nz), jnp.float32)
        if rel is None:
            clear()
        else:
            pl.when(jnp.logical_not(inside(rel)))(clear)
    started = []
    for index, part, dest, lo, rel in copies:
        source = ins[index]
        if part == "orb":
            source = source.at[pl.ds(0, block_count)]
        elif part == "pot":
            source = source.at[block_count]
        elif isinstance(part, int):
            source = source.at[part]
        elif isinstance(part, tuple):
            source = source.at[pl.ds(part[0], part[1])]
        if dest == "cells":
            target = cells_ref.at[:, pl.ds(lo, source.shape[1])]
        else:
            target = pot_ref.at[pl.ds(lo, source.shape[0])]
        copy = pltpu.make_async_copy(source, target, sems.at[len(started)])
        if rel is None:
            copy.start()
        else:
            pl.when(inside(rel))(copy.start)
        started.append((copy, rel))
    for copy, rel in started:
        if rel is None:
            copy.wait()
        else:
            pl.when(inside(rel))(copy.wait)

    sources = (cells_ref,) + tuple(iter_refs)

    def plane_value(order, b, p):
        source = sources[order - 1]
        field = source[b, RADIUS + p]
        laplace = (3.0 * CENTER_COEF) * field
        for offset, weight in enumerate(STENCIL, 1):
            beside_all = source[b, RADIUS + p + offset] + source[b, RADIUS + p - offset]
            beside_all = beside_all + pltpu.roll(field, offset, 0) + pltpu.roll(field, ny - offset, 0)
            laplace = laplace + weight * beside_all
        laplace = laplace + zsum_ref[b, p]
        applied = -0.5 * laplace + pot_ref[(order - 1) * RADIUS + p] * field
        if order == 1:
            return (applied - SHIFT_C * field) / HALF_W
        before = sources[order - 2][b, 2 * RADIUS + p]
        return 2.0 * (applied - SHIFT_C * field) / HALF_W - before

    def along_z(order, planes):
        source = sources[order - 1]
        for b in range(block_orbs):
            rows = source[b, RADIUS : RADIUS + planes].reshape(planes * ny, nz)
            mixed = jnp.dot(rows, cz_ref[...], precision=lax.Precision.HIGHEST, preferred_element_type=jnp.float32)
            zsum_ref[b, :planes] = mixed.reshape(planes, ny, nz)

    for order in range(1, DEG_MAX):
        margin = (DEG_MAX - order) * RADIUS
        dest = iter_refs[order - 1]
        planes = slab + 2 * margin
        along_z(order, planes)
        for b in range(block_orbs):
            def body(p, carry, order=order, b=b, dest=dest):
                value = plane_value(order, b, p)
                plane = first + order * RADIUS + p
                keep = jnp.full((ny, nz), plane, jnp.int32)
                keep = (keep >= 0) & (keep < grid_planes)
                dest[b, p] = jnp.where(keep, value, 0.0)
                return carry
            lax.fori_loop(0, planes, body, 0, unroll=2)

    along_z(DEG_MAX, slab)
    for b in range(block_orbs):
        def last(p, carry, b=b):
            value = plane_value(DEG_MAX, b, p)
            levels = jnp.full((ny, nz), degree, jnp.int32)
            picked = iter_refs[0][b, (DEG_MAX - 1) * RADIUS + p]
            for order in range(2, DEG_MAX):
                picked = jnp.where(levels >= order, iter_refs[order - 1][b, (DEG_MAX - order) * RADIUS + p], picked)
            picked = jnp.where(levels >= DEG_MAX, value, picked)
            out_ref[b, p] = picked.astype(out_ref.dtype)
            return carry
        lax.fori_loop(0, slab, last, 0, unroll=2)


def filter_call(operands, copies, zeros, first, degree, grid_planes, block_orbs, slab, ny, nz):
    reach = DEG_MAX * RADIUS
    smem = pl.BlockSpec(memory_space=pltpu.SMEM)
    hbm = pl.BlockSpec(memory_space=pl.ANY)
    vmem = pl.BlockSpec(memory_space=pltpu.VMEM)
    planes = sum(block_orbs * (slab + 2 * (DEG_MAX - order) * RADIUS) for order in range(1, DEG_MAX + 1))
    cost = pl.CostEstimate(
        flops=planes * ny * nz * (2 * nz * 6 + 40),
        transcendentals=0,
        bytes_accessed=4 * ny * nz * (block_orbs * (slab + 2 * reach) + slab + 2 * (reach - RADIUS)),
    )
    return pl.pallas_call(
        functools.partial(
            filter_kernel,
            copies=tuple(copies),
            zeros=tuple(zeros),
            n_in=len(operands),
            block_count=block_orbs,
            grid_planes=grid_planes,
        ),
        out_shape=jax.ShapeDtypeStruct((block_orbs, slab, ny, nz), jnp.bfloat16),
        in_specs=[smem, smem, vmem] + [hbm] * len(operands),
        out_specs=vmem,
        scratch_shapes=[
            pltpu.VMEM((block_orbs, slab + 2 * reach, ny, nz), jnp.float32),
            pltpu.VMEM((slab + 2 * (reach - RADIUS), ny, nz), jnp.float32),
            pltpu.VMEM((block_orbs, slab + 2 * (reach - RADIUS), ny, nz), jnp.float32),
            pltpu.SemaphoreType.DMA((len(copies),)),
        ]
        + [
            pltpu.VMEM((block_orbs, slab + 2 * (DEG_MAX - order) * RADIUS, ny, nz), jnp.float32)
            for order in range(1, DEG_MAX)
        ],
        cost_estimate=cost,
    )(first, degree, jnp.asarray(circulant(nz)), *operands)


def chebyshev_filter(orbitals, potential, first, degree, grid_planes):
    block_orbs, slab, ny, nz = orbitals.shape
    reach = DEG_MAX * RADIUS
    pot_reach = reach - RADIUS
    args = (first, degree, grid_planes)
    if reach % slab or pot_reach % slab or lax.axis_size("dom") - 1 > reach // slab:
        operands, copies, zeros = halo_plan(orbitals, potential, reach, pot_reach)
        return filter_call(operands, copies, zeros, *args, block_orbs, slab, ny, nz)
    local = [(0, "all", "cells", reach, None), (1, "all", "pot", pot_reach, None)]
    pieces = cyclic_gather(jnp.concatenate([orbitals[:1], potential[None]], axis=0))
    later = [cyclic_gather(orbitals[i : i + 1]) for i in range(1, block_orbs)]
    outs = []
    for i in range(block_orbs):
        own = pieces if i == 0 else later[i - 1] + pieces
        copies, zeros = gather_copies(2, 2 + len(own) - len(pieces), 1, reach, pot_reach, slab)
        operands = [orbitals[i : i + 1], potential] + own
        outs.append(filter_call(operands, local + copies, zeros, *args, 1, slab, ny, nz))
    return jnp.concatenate(outs, axis=0)


def inner_rows(left, right):
    return lax.dot_general(
        left, right, (((1,), (1,)), ((), ())), preferred_element_type=jnp.float32
    )


def per_device(orbitals, potential, degrees):
    block_orbs, slab = orbitals.shape[0], orbitals.shape[1]
    n_orb, n_dom = lax.axis_size("orb"), lax.axis_size("dom")
    grid_planes = slab * n_dom
    start = lax.axis_index("dom") * slab
    first = (start - DEG_MAX * RADIUS).astype(jnp.int32).reshape(1)
    filtered = chebyshev_filter(orbitals, potential, first, degrees.astype(jnp.int32), grid_planes)
    cell_count = orbitals.shape[1] * orbitals.shape[2] * orbitals.shape[3]
    total_cells = float(cell_count * n_dom)
    flattened = filtered.reshape(block_orbs, cell_count)
    mixed = lax.all_to_all(flattened, "orb", split_axis=1, concat_axis=0, tiled=True)
    partial_gram = inner_rows(mixed, mixed)
    rows = partial_gram.reshape(n_orb, 1, block_orbs, -1)
    sends = jnp.broadcast_to(rows, (n_orb, n_dom) + rows.shape[2:]).reshape((n_orb * n_dom,) + rows.shape[2:])
    gathered = lax.all_to_all(sends, ("orb", "dom"), split_axis=0, concat_axis=0, tiled=True)
    correlation = gathered.sum(axis=0) / total_cells
    return (filtered, correlation)


def solution(mesh):
    placed = (P("orb", "dom", None, None), P("dom", None, None), P("orb"))
    return jax.shard_map(
        per_device,
        mesh=mesh,
        in_specs=placed,
        out_specs=(P("orb", "dom", None, None), P("orb", None)),
        check_vma=False,
    )
```

```python
import functools

import numpy as np
import jax
import jax.numpy as jnp
from jax import lax
from jax.experimental import pallas as pl
from jax.experimental.pallas import tpu as pltpu
from jax.sharding import PartitionSpec as P


DEG_MAX = 3


CENTER_COEF = -5369.0 / 1800.0
STENCIL = (12.0 / 7.0, -15.0 / 56.0, 10.0 / 189.0, -1.0 / 112.0, 2.0 / 1925.0, -1.0 / 16632.0)
SHIFT_C = 8.5
HALF_W = 4.5
RADIUS = len(STENCIL)


def circulant(n):
    gap = (np.arange(n)[None, :] - np.arange(n)[:, None]) % n
    weights = np.zeros((n, n), np.float32)
    for offset, weight in enumerate(STENCIL, 1):
        weights[(gap == offset) | (gap == n - offset)] = np.float32(weight)
    return weights


def shifted(x, k):
    count = lax.axis_size("dom")
    pairs = [(i, i + k) for i in range(count) if 0 <= i + k < count]
    if not pairs:
        return jnp.zeros_like(x)
    return lax.ppermute(x, "dom", pairs)


def cyclic_gather(send):
    count = lax.axis_size("dom")
    return [lax.ppermute(send, "dom", [(i, (i + k) % count) for i in range(count)]) for k in range(1, count)]


def gather_copies(first_piece, pot_first_piece, pot_row, reach, pot_reach, slab):
    count = lax.axis_size("dom")
    copies, zeros = [], []
    for rel in range(-(reach // slab), reach // slab + 1):
        if rel == 0:
            continue
        k = (-rel) % count
        if k == 0:
            zeros.append(("cells", reach + rel * slab, None))
        else:
            copies.append((first_piece + k - 1, (0, 1), "cells", reach + rel * slab, rel))
            zeros.append(("cells", reach + rel * slab, rel))
        if abs(rel) * slab <= pot_reach:
            if k == 0:
                zeros.append(("pot", pot_reach + rel * slab, None))
            else:
                copies.append((pot_first_piece + k - 1, pot_row, "pot", pot_reach + rel * slab, rel))
                zeros.append(("pot", pot_reach + rel * slab, rel))
    return copies, zeros


def halo_plan(orbitals, potential, reach, pot_reach):
    slab = orbitals.shape[1]
    operands = [orbitals, potential]
    copies = [(0, "all", "cells", reach, None), (1, "all", "pot", pot_reach, None)]
    packed = None
    k = 1
    while slab * (k - 1) < reach:
        count = min(slab, reach - slab * (k - 1))
        pot_count = max(0, min(slab, pot_reach - slab * (k - 1)))
        for sign in (1, -1):
            if pot_count == slab and count == slab:
                if packed is None:
                    packed = jnp.concatenate([orbitals, potential[None]], axis=0)
                parts = [(packed, "orb", count, "cells", reach), (None, "pot", count, "pot", pot_reach)]
            else:
                parts = [(orbitals, "all", count, "cells", reach)]
                if pot_count:
                    parts.append((potential, "all", pot_count, "pot", pot_reach))
            for values, part, size, dest, centre in parts:
                lo = centre - slab * (k - 1) - size if sign > 0 else centre + slab * k
                if values is not None:
                    axis = 0 if values is potential else 1
                    span = values.shape[axis]
                    if sign > 0:
                        piece = lax.slice_in_dim(values, span - size, span, axis=axis)
                    else:
                        piece = lax.slice_in_dim(values, 0, size, axis=axis)
                    operands.append(shifted(piece, sign * k))
                copies.append((len(operands) - 1, part, dest, lo, None))
        k += 1
    return operands, copies, []


def filter_kernel(first_ref, deg_ref, cz_ref, *refs, copies, zeros, n_in, block_count, grid_planes):
    ins = refs[:n_in]
    out_ref = refs[n_in]
    cells_ref, pot_ref, zsum_ref, sems = refs[n_in + 1 : n_in + 5]
    iter_refs = refs[n_in + 5 :]
    block_orbs, _, ny, nz = cells_ref.shape
    slab = out_ref.shape[1]
    first = first_ref[0]
    degree = deg_ref[0]

    reach = DEG_MAX * RADIUS
    own_slab = (first + reach) // slab

    def inside(rel):
        return (own_slab + rel >= 0) & (own_slab + rel < grid_planes // slab)

    for dest, lo, rel in zeros:
        def clear(dest=dest, lo=lo):
            if dest == "cells":
                cells_ref[:, pl.ds(lo, slab)] = jnp.zeros((block_orbs, slab, ny, nz), jnp.float32)
            else:
                pot_ref[pl.ds(lo, slab)] = jnp.zeros((slab, ny, nz), jnp.float32)

        if rel is None:
            clear()
        else:
            pl.when(jnp.logical_not(inside(rel)))(clear)
    started = []
    for index, part, dest, lo, rel in copies:
        source = ins[index]
        if part == "orb":
            source = source.at[pl.ds(0, block_count)]
        elif part == "pot":
            source = source.at[block_count]
        elif isinstance(part, int):
            source = source.at[part]
        elif isinstance(part, tuple):
            source = source.at[pl.ds(part[0], part[1])]
        if dest == "cells":
            target = cells_ref.at[:, pl.ds(lo, source.shape[1])]
        else:
            target = pot_ref.at[pl.ds(lo, source.shape[0])]
        copy = pltpu.make_async_copy(source, target, sems.at[len(started)])
        if rel is None:
            copy.start()
        else:
            pl.when(inside(rel))(copy.start)
        started.append((copy, rel))
    for copy, rel in started:
        if rel is None:
            copy.wait()
        else:
            pl.when(inside(rel))(copy.wait)

    sources = (cells_ref,) + tuple(iter_refs)

    def plane_value(order, b, p):
        source = sources[order - 1]
        field = source[b, RADIUS + p]
        laplace = (3.0 * CENTER_COEF) * field
        for offset, weight in enumerate(STENCIL, 1):
            beside_all = source[b, RADIUS + p + offset] + source[b, RADIUS + p - offset]
            beside_all = beside_all + pltpu.roll(field, offset, 0) + pltpu.roll(field, ny - offset, 0)
            laplace = laplace + weight * beside_all
        laplace = laplace + zsum_ref[b, p]
        applied = -0.5 * laplace + pot_ref[(order - 1) * RADIUS + p] * field
        if order == 1:
            return (applied - SHIFT_C * field) / HALF_W
        before = sources[order - 2][b, 2 * RADIUS + p]
        return 2.0 * (applied - SHIFT_C * field) / HALF_W - before

    def along_z(order, planes):
        source = sources[order - 1]
        for b in range(block_orbs):
            rows = source[b, RADIUS : RADIUS + planes].reshape(planes * ny, nz)
            mixed = jnp.dot(rows, cz_ref[...], precision=lax.Precision.HIGHEST, preferred_element_type=jnp.float32)
            zsum_ref[b, :planes] = mixed.reshape(planes, ny, nz)

    for order in range(1, DEG_MAX):
        margin = (DEG_MAX - order) * RADIUS
        dest = iter_refs[order - 1]
        planes = slab + 2 * margin
        along_z(order, planes)
        for b in range(block_orbs):
            def body(p, carry, order=order, b=b, dest=dest):
                value = plane_value(order, b, p)
                plane = first + order * RADIUS + p
                keep = jnp.full((ny, nz), plane, jnp.int32)
                keep = (keep >= 0) & (keep < grid_planes)
                dest[b, p] = jnp.where(keep, value, 0.0)
                return carry

            lax.fori_loop(0, planes, body, 0, unroll=2)

    along_z(DEG_MAX, slab)
    for b in range(block_orbs):
        def last(p, carry, b=b):
            value = plane_value(DEG_MAX, b, p)
            levels = jnp.full((ny, nz), degree, jnp.int32)
            picked = iter_refs[0][b, (DEG_MAX - 1) * RADIUS + p]
            for order in range(2, DEG_MAX):
                picked = jnp.where(levels >= order, iter_refs[order - 1][b, (DEG_MAX - order) * RADIUS + p], picked)
            picked = jnp.where(levels >= DEG_MAX, value, picked)
            out_ref[b, p] = picked.astype(out_ref.dtype)
            return carry

        lax.fori_loop(0, slab, last, 0, unroll=2)


def filter_call(operands, copies, zeros, first, degree, grid_planes, block_orbs, slab, ny, nz):
    reach = DEG_MAX * RADIUS
    smem = pl.BlockSpec(memory_space=pltpu.SMEM)
    hbm = pl.BlockSpec(memory_space=pl.ANY)
    vmem = pl.BlockSpec(memory_space=pltpu.VMEM)
    planes = sum(block_orbs * (slab + 2 * (DEG_MAX - order) * RADIUS) for order in range(1, DEG_MAX + 1))
    cost = pl.CostEstimate(
        flops=planes * ny * nz * (2 * nz * 6 + 40),
        transcendentals=0,
        bytes_accessed=4 * ny * nz * (block_orbs * (slab + 2 * reach) + slab + 2 * (reach - RADIUS)),
    )
    return pl.pallas_call(
        functools.partial(
            filter_kernel,
            copies=tuple(copies),
            zeros=tuple(zeros),
            n_in=len(operands),
            block_count=block_orbs,
            grid_planes=grid_planes,
        ),
        out_shape=jax.ShapeDtypeStruct((block_orbs, slab, ny, nz), jnp.bfloat16),
        in_specs=[smem, smem, vmem] + [hbm] * len(operands),
        out_specs=vmem,
        scratch_shapes=[
            pltpu.VMEM((block_orbs, slab + 2 * reach, ny, nz), jnp.float32),
            pltpu.VMEM((slab + 2 * (reach - RADIUS), ny, nz), jnp.float32),
            pltpu.VMEM((block_orbs, slab + 2 * (reach - RADIUS), ny, nz), jnp.float32),
            pltpu.SemaphoreType.DMA((len(copies),)),
        ]
        + [
            pltpu.VMEM((block_orbs, slab + 2 * (DEG_MAX - order) * RADIUS, ny, nz), jnp.float32)
            for order in range(1, DEG_MAX)
        ],
        cost_estimate=cost,
    )(first, degree, jnp.asarray(circulant(nz)), *operands)


def chebyshev_filter(orbitals, potential, first, degree, grid_planes):
    block_orbs, slab, ny, nz = orbitals.shape
    reach = DEG_MAX * RADIUS
    pot_reach = reach - RADIUS
    args = (first, degree, grid_planes)
    if reach % slab or pot_reach % slab or lax.axis_size("dom") - 1 > reach // slab:
        operands, copies, zeros = halo_plan(orbitals, potential, reach, pot_reach)
        return [filter_call(operands, copies, zeros, *args, block_orbs, slab, ny, nz)]
    local = [(0, "all", "cells", reach, None), (1, "all", "pot", pot_reach, None)]
    pieces = cyclic_gather(jnp.concatenate([orbitals[:1], potential[None]], axis=0))
    later = []
    for i in range(1, block_orbs):
        later.append(cyclic_gather(orbitals[i : i + 1]))
    outs = []
    for i in range(block_orbs):
        own = pieces if i == 0 else later[i - 1] + pieces
        copies, zeros = gather_copies(2, 2 + len(own) - len(pieces), 1, reach, pot_reach, slab)
        operands = [orbitals[i : i + 1], potential] + own + outs[-1:]
        outs.append(filter_call(operands, local + copies, zeros, *args, 1, slab, ny, nz))
    return outs


def inner_rows(left, right):
    return lax.dot_general(
        left, right, (((1,), (1,)), ((), ())), preferred_element_type=jnp.float32
    )


def per_device(orbitals, potential, degrees):
    block_orbs, slab = orbitals.shape[0], orbitals.shape[1]
    n_orb, n_dom = lax.axis_size("orb"), lax.axis_size("dom")
    grid_planes = slab * n_dom
    start = lax.axis_index("dom") * slab
    first = (start - DEG_MAX * RADIUS).astype(jnp.int32).reshape(1)
    filtered = chebyshev_filter(orbitals, potential, first, degrees.astype(jnp.int32), grid_planes)
    cell_count = orbitals.shape[1] * orbitals.shape[2] * orbitals.shape[3]
    total_cells = float(cell_count * n_dom)
    parts = []
    for part in filtered:
        parts.append(
            lax.all_to_all(part.reshape(part.shape[0], cell_count), "orb", split_axis=1, concat_axis=0, tiled=True)
        )
    mixed = jnp.stack([part.reshape(n_orb, -1, part.shape[-1]) for part in parts], axis=1)
    mixed = mixed.reshape(n_orb * block_orbs, -1)
    filtered = jnp.concatenate(filtered, axis=0)
    partial_gram = inner_rows(mixed, mixed)
    rows = partial_gram.reshape(n_orb, 1, block_orbs, -1)
    sends = jnp.broadcast_to(rows, (n_orb, n_dom) + rows.shape[2:]).reshape((n_orb * n_dom,) + rows.shape[2:])
    gathered = lax.all_to_all(sends, ("orb", "dom"), split_axis=0, concat_axis=0, tiled=True)
    correlation = gathered.sum(axis=0) / total_cells
    return (filtered, correlation)


def solution(mesh):
    placed = (P("orb", "dom", None, None), P("dom", None, None), P("orb"))
    return jax.shard_map(
        per_device,
        mesh=mesh,
        in_specs=placed,
        out_specs=(P("orb", "dom", None, None), P("orb", None)),
        check_vma=False,
    )
```

```python
import functools

import numpy as np
import jax
import jax.numpy as jnp
from jax import lax
from jax.experimental import pallas as pl
from jax.experimental.pallas import tpu as pltpu
from jax.sharding import PartitionSpec as P

DEG_MAX = 3


CENTER_COEF = -5369.0 / 1800.0
STENCIL = (12.0 / 7.0, -15.0 / 56.0, 10.0 / 189.0, -1.0 / 112.0, 2.0 / 1925.0, -1.0 / 16632.0)
SHIFT_C = 8.5
HALF_W = 4.5
RADIUS = len(STENCIL)


def circulant(n):
    gap = (np.arange(n)[None, :] - np.arange(n)[:, None]) % n
    weights = np.zeros((n, n), np.float32)
    for offset, weight in enumerate(STENCIL, 1):
        weights[(gap == offset) | (gap == n - offset)] = np.float32(weight)
    return weights


def shifted(x, k):
    count = lax.axis_size("dom")
    pairs = [(i, i + k) for i in range(count) if 0 <= i + k < count]
    if not pairs:
        return jnp.zeros_like(x)
    return lax.ppermute(x, "dom", pairs)


def gather_plan(orbitals, potential, reach, pot_reach):
    block_orbs, slab = orbitals.shape[0], orbitals.shape[1]
    count = lax.axis_size("dom")
    packed = jnp.concatenate([orbitals, potential[None]], axis=0)
    operands = [orbitals, potential]
    copies = [(0, "all", "cells", reach, None), (1, "all", "pot", pot_reach, None)]
    zeros = []
    pairwise = count & (count - 1) == 0
    for k in range(1, count):
        source = [j ^ k if pairwise else (j - k) % count for j in range(count)]
        near = [j for j in range(count) if abs(source[j] - j) * slab <= pot_reach]
        far = [j for j in range(count) if j not in near]
        for group, values, with_pot in ((near, packed, True), (far, orbitals, False)):
            if not group:
                continue
            operands.append(lax.ppermute(values, "dom", [(source[j], j) for j in group]))
            for rel in sorted({source[j] - j for j in group}):
                devices = tuple(j for j in group if source[j] - j == rel)
                copies.append((len(operands) - 1, "orb" if with_pot else "all", "cells", reach + rel * slab, devices))
                if with_pot:
                    copies.append((len(operands) - 1, "pot", "pot", pot_reach + rel * slab, devices))
    for rel in range(-(reach // slab), reach // slab + 1):
        if rel != 0:
            zeros.append(("cells", reach + rel * slab, rel))
            if abs(rel) * slab <= pot_reach:
                zeros.append(("pot", pot_reach + rel * slab, rel))
    return operands, copies, zeros


def halo_plan(orbitals, potential, reach, pot_reach):
    block_orbs, slab = orbitals.shape[0], orbitals.shape[1]
    if reach % slab == 0 and pot_reach % slab == 0 and lax.axis_size("dom") - 1 <= reach // slab:
        return gather_plan(orbitals, potential, reach, pot_reach)
    operands = [orbitals, potential]
    copies = [(0, "all", "cells", reach, None), (1, "all", "pot", pot_reach, None)]
    packed = None
    k = 1
    while slab * (k - 1) < reach:
        count = min(slab, reach - slab * (k - 1))
        pot_count = max(0, min(slab, pot_reach - slab * (k - 1)))
        for sign in (1, -1):
            if pot_count == slab and count == slab:
                if packed is None:
                    packed = jnp.concatenate([orbitals, potential[None]], axis=0)
                parts = [(packed, "orb", count, "cells", reach), (None, "pot", count, "pot", pot_reach)]
            else:
                parts = [(orbitals, "all", count, "cells", reach)]
                if pot_count:
                    parts.append((potential, "all", pot_count, "pot", pot_reach))
            for values, part, size, dest, centre in parts:
                lo = centre - slab * (k - 1) - size if sign > 0 else centre + slab * k
                if values is not None:
                    axis = 0 if values is potential else 1
                    span = values.shape[axis]
                    if sign > 0:
                        piece = lax.slice_in_dim(values, span - size, span, axis=axis)
                    else:
                        piece = lax.slice_in_dim(values, 0, size, axis=axis)
                    operands.append(shifted(piece, sign * k))
                copies.append((len(operands) - 1, part, dest, lo, None))
        k += 1
    return operands, copies, []


def filter_kernel(first_ref, deg_ref, cz_ref, *refs, copies, zeros, n_in, block_count, grid_planes):
    ins = refs[:n_in]
    out_ref = refs[n_in]
    cells_ref, pot_ref, zsum_ref, sems = refs[n_in + 1 : n_in + 5]
    iter_refs = refs[n_in + 5 :]
    block_orbs, _, ny, nz = cells_ref.shape
    slab = out_ref.shape[1]
    first = first_ref[0]
    degree = deg_ref[0]

    reach = DEG_MAX * RADIUS
    own_slab = (first + reach) // slab

    def inside(rel):
        return (own_slab + rel >= 0) & (own_slab + rel < grid_planes // slab)

    for dest, lo, rel in zeros:
        def clear(dest=dest, lo=lo):
            if dest == "cells":
                cells_ref[:, pl.ds(lo, slab)] = jnp.zeros((block_orbs, slab, ny, nz), jnp.float32)
            else:
                pot_ref[pl.ds(lo, slab)] = jnp.zeros((slab, ny, nz), jnp.float32)
        pl.when(jnp.logical_not(inside(rel)))(clear)
    def chosen(devices):
        hit = own_slab == devices[0]
        for device in devices[1:]:
            hit = hit | (own_slab == device)
        return hit

    started = []
    for index, part, dest, lo, rel in copies:
        source = ins[index]
        if part == "orb":
            source = source.at[pl.ds(0, block_count)]
        elif part == "pot":
            source = source.at[block_count]
        if dest == "cells":
            target = cells_ref.at[:, pl.ds(lo, source.shape[1])]
        else:
            target = pot_ref.at[pl.ds(lo, source.shape[0])]
        copy = pltpu.make_async_copy(source, target, sems.at[len(started)])
        if rel is None:
            copy.start()
        else:
            pl.when(chosen(rel))(copy.start)
        started.append((copy, rel))
    for copy, rel in started:
        if rel is None:
            copy.wait()
        else:
            pl.when(chosen(rel))(copy.wait)

    sources = (cells_ref,) + tuple(iter_refs)

    def plane_value(order, b, p):
        source = sources[order - 1]
        field = source[b, RADIUS + p]
        laplace = (3.0 * CENTER_COEF) * field
        for offset, weight in enumerate(STENCIL, 1):
            beside_all = source[b, RADIUS + p + offset] + source[b, RADIUS + p - offset]
            beside_all = beside_all + pltpu.roll(field, offset, 0) + pltpu.roll(field, ny - offset, 0)
            laplace = laplace + weight * beside_all
        laplace = laplace + zsum_ref[b, p]
        applied = -0.5 * laplace + pot_ref[(order - 1) * RADIUS + p] * field
        if order == 1:
            return (applied - SHIFT_C * field) / HALF_W
        before = sources[order - 2][b, 2 * RADIUS + p]
        return 2.0 * (applied - SHIFT_C * field) / HALF_W - before

    def along_z(order, planes):
        source = sources[order - 1]
        for b in range(block_orbs):
            rows = source[b, RADIUS : RADIUS + planes].reshape(planes * ny, nz)
            mixed = jnp.dot(rows, cz_ref[...], precision=lax.Precision.HIGHEST, preferred_element_type=jnp.float32)
            zsum_ref[b, :planes] = mixed.reshape(planes, ny, nz)

    for order in range(1, DEG_MAX):
        margin = (DEG_MAX - order) * RADIUS
        dest = iter_refs[order - 1]
        planes = slab + 2 * margin
        along_z(order, planes)
        for b in range(block_orbs):
            def body(p, carry, order=order, b=b, dest=dest):
                value = plane_value(order, b, p)
                plane = first + order * RADIUS + p
                keep = jnp.full((ny, nz), plane, jnp.int32)
                keep = (keep >= 0) & (keep < grid_planes)
                dest[b, p] = jnp.where(keep, value, 0.0)
                return carry
            lax.fori_loop(0, planes, body, 0, unroll=2)

    along_z(DEG_MAX, slab)
    for b in range(block_orbs):
        def last(p, carry, b=b):
            value = plane_value(DEG_MAX, b, p)
            levels = jnp.full((ny, nz), degree, jnp.int32)
            picked = iter_refs[0][b, (DEG_MAX - 1) * RADIUS + p]
            for order in range(2, DEG_MAX):
                picked = jnp.where(levels >= order, iter_refs[order - 1][b, (DEG_MAX - order) * RADIUS + p], picked)
            picked = jnp.where(levels >= DEG_MAX, value, picked)
            out_ref[b, p] = picked.astype(out_ref.dtype)
            return carry
        lax.fori_loop(0, slab, last, 0, unroll=2)


def chebyshev_filter(orbitals, potential, first, degree, grid_planes):
    block_orbs, slab, ny, nz = orbitals.shape
    reach = DEG_MAX * RADIUS
    operands, copies, zeros = halo_plan(orbitals, potential, reach, reach - RADIUS)
    smem = pl.BlockSpec(memory_space=pltpu.SMEM)
    hbm = pl.BlockSpec(memory_space=pl.ANY)
    vmem = pl.BlockSpec(memory_space=pltpu.VMEM)
    return pl.pallas_call(
        functools.partial(
            filter_kernel,
            copies=tuple(copies),
            zeros=tuple(zeros),
            n_in=len(operands),
            block_count=block_orbs,
            grid_planes=grid_planes,
        ),
        out_shape=jax.ShapeDtypeStruct((block_orbs, slab, ny, nz), jnp.bfloat16),
        in_specs=[smem, smem, vmem] + [hbm] * len(operands),
        out_specs=vmem,
        scratch_shapes=[
            pltpu.VMEM((block_orbs, slab + 2 * reach, ny, nz), jnp.float32),
            pltpu.VMEM((slab + 2 * (reach - RADIUS), ny, nz), jnp.float32),
            pltpu.VMEM((block_orbs, slab + 2 * (reach - RADIUS), ny, nz), jnp.float32),
            pltpu.SemaphoreType.DMA((len(copies),)),
        ]
        + [
            pltpu.VMEM((block_orbs, slab + 2 * (DEG_MAX - order) * RADIUS, ny, nz), jnp.float32)
            for order in range(1, DEG_MAX)
        ],
    )(first, degree, jnp.asarray(circulant(nz)), *operands)


def inner_rows(left, right):
    return lax.dot_general(
        left, right, (((1,), (1,)), ((), ())), preferred_element_type=jnp.float32
    )


def per_device(orbitals, potential, degrees):
    block_orbs, slab = orbitals.shape[0], orbitals.shape[1]
    n_orb, n_dom = lax.axis_size("orb"), lax.axis_size("dom")
    grid_planes = slab * n_dom
    start = lax.axis_index("dom") * slab
    first = (start - DEG_MAX * RADIUS).astype(jnp.int32).reshape(1)
    filtered = chebyshev_filter(orbitals, potential, first, degrees.astype(jnp.int32), grid_planes)
    cell_count = orbitals.shape[1] * orbitals.shape[2] * orbitals.shape[3]
    total_cells = float(cell_count * n_dom)
    flattened = filtered.reshape(block_orbs, cell_count)
    mixed = lax.all_to_all(flattened, "orb", split_axis=1, concat_axis=0, tiled=True)
    partial_gram = inner_rows(mixed, mixed)
    rows = partial_gram.reshape(n_orb, 1, block_orbs, -1)
    sends = jnp.broadcast_to(rows, (n_orb, n_dom) + rows.shape[2:]).reshape((n_orb * n_dom,) + rows.shape[2:])
    gathered = lax.all_to_all(sends, ("orb", "dom"), split_axis=0, concat_axis=0, tiled=True)
    correlation = gathered.sum(axis=0) / total_cells
    return (filtered, correlation)


def solution(mesh):
    placed = (P("orb", "dom", None, None), P("dom", None, None), P("orb"))
    return jax.shard_map(
        per_device,
        mesh=mesh,
        in_specs=placed,
        out_specs=(P("orb", "dom", None, None), P("orb", None)),
        check_vma=False,
    )
```

```python
import functools

import numpy as np
import jax
import jax.numpy as jnp
from jax import lax
from jax.experimental import pallas as pl
from jax.experimental.pallas import tpu as pltpu
from jax.sharding import PartitionSpec as P

DEG_MAX = 3


CENTER_COEF = -5369.0 / 1800.0
STENCIL = (12.0 / 7.0, -15.0 / 56.0, 10.0 / 189.0, -1.0 / 112.0, 2.0 / 1925.0, -1.0 / 16632.0)
SHIFT_C = 8.5
HALF_W = 4.5
RADIUS = len(STENCIL)


def circulant(n):
    gap = (np.arange(n)[None, :] - np.arange(n)[:, None]) % n
    weights = np.zeros((n, n), np.float32)
    for offset, weight in enumerate(STENCIL, 1):
        weights[(gap == offset) | (gap == n - offset)] = np.float32(weight)
    return weights


def shifted(x, k):
    count = lax.axis_size("dom")
    pairs = [(i, i + k) for i in range(count) if 0 <= i + k < count]
    if not pairs:
        return jnp.zeros_like(x)
    return lax.ppermute(x, "dom", pairs)


def gather_plan(orbitals, potential, reach, pot_reach):
    block_orbs, slab = orbitals.shape[0], orbitals.shape[1]
    count = lax.axis_size("dom")
    packed = jnp.concatenate([orbitals, potential[None]], axis=0)
    operands = [orbitals, potential]
    copies = [(0, "all", "cells", reach, None), (1, "all", "pot", pot_reach, None)]
    zeros = []
    pairwise = count & (count - 1) == 0
    for k in range(1, count):
        source = [j ^ k if pairwise else (j - k) % count for j in range(count)]
        near = [j for j in range(count) if abs(source[j] - j) * slab <= pot_reach]
        far = [j for j in range(count) if j not in near]
        for group, values, with_pot in ((near, packed, True), (far, orbitals, False)):
            if not group:
                continue
            operands.append(lax.ppermute(values, "dom", [(source[j], j) for j in group]))
            for rel in sorted({source[j] - j for j in group}):
                devices = tuple(j for j in group if source[j] - j == rel)
                copies.append((len(operands) - 1, "orb" if with_pot else "all", "cells", reach + rel * slab, devices))
                if with_pot:
                    copies.append((len(operands) - 1, "pot", "pot", pot_reach + rel * slab, devices))
    for rel in range(-(reach // slab), reach // slab + 1):
        if rel != 0:
            zeros.append(("cells", reach + rel * slab, rel))
            if abs(rel) * slab <= pot_reach:
                zeros.append(("pot", pot_reach + rel * slab, rel))
    return operands, copies, zeros


def halo_plan(orbitals, potential, reach, pot_reach):
    block_orbs, slab = orbitals.shape[0], orbitals.shape[1]
    if reach % slab == 0 and pot_reach % slab == 0 and lax.axis_size("dom") - 1 <= reach // slab:
        return gather_plan(orbitals, potential, reach, pot_reach)
    operands = [orbitals, potential]
    copies = [(0, "all", "cells", reach, None), (1, "all", "pot", pot_reach, None)]
    packed = None
    k = 1
    while slab * (k - 1) < reach:
        count = min(slab, reach - slab * (k - 1))
        pot_count = max(0, min(slab, pot_reach - slab * (k - 1)))
        for sign in (1, -1):
            if pot_count == slab and count == slab:
                if packed is None:
                    packed = jnp.concatenate([orbitals, potential[None]], axis=0)
                parts = [(packed, "orb", count, "cells", reach), (None, "pot", count, "pot", pot_reach)]
            else:
                parts = [(orbitals, "all", count, "cells", reach)]
                if pot_count:
                    parts.append((potential, "all", pot_count, "pot", pot_reach))
            for values, part, size, dest, centre in parts:
                lo = centre - slab * (k - 1) - size if sign > 0 else centre + slab * k
                if values is not None:
                    axis = 0 if values is potential else 1
                    span = values.shape[axis]
                    if sign > 0:
                        piece = lax.slice_in_dim(values, span - size, span, axis=axis)
                    else:
                        piece = lax.slice_in_dim(values, 0, size, axis=axis)
                    operands.append(shifted(piece, sign * k))
                copies.append((len(operands) - 1, part, dest, lo, None))
        k += 1
    return operands, copies, []


def filter_kernel(first_ref, deg_ref, cz_ref, *refs, copies, zeros, n_in, block_count, grid_planes):
    ins = refs[:n_in]
    out_ref = refs[n_in]
    cells_ref, pot_ref, zsum_ref, sems = refs[n_in + 1 : n_in + 5]
    iter_refs = refs[n_in + 5 :]
    block_orbs, _, ny, nz = cells_ref.shape
    slab = out_ref.shape[1]
    first = first_ref[0]
    degree = deg_ref[0]

    reach = DEG_MAX * RADIUS
    own_slab = (first + reach) // slab

    def inside(rel):
        return (own_slab + rel >= 0) & (own_slab + rel < grid_planes // slab)

    for dest, lo, rel in zeros:
        def clear(dest=dest, lo=lo):
            if dest == "cells":
                cells_ref[:, pl.ds(lo, slab)] = jnp.zeros((block_orbs, slab, ny, nz), jnp.float32)
            else:
                pot_ref[pl.ds(lo, slab)] = jnp.zeros((slab, ny, nz), jnp.float32)
        pl.when(jnp.logical_not(inside(rel)))(clear)
    def chosen(devices):
        hit = own_slab == devices[0]
        for device in devices[1:]:
            hit = hit | (own_slab == device)
        return hit

    started = []
    for index, part, dest, lo, rel in copies:
        source = ins[index]
        if part == "orb":
            source = source.at[pl.ds(0, block_count)]
        elif part == "pot":
            source = source.at[block_count]
        if dest == "cells":
            target = cells_ref.at[:, pl.ds(lo, source.shape[1])]
        else:
            target = pot_ref.at[pl.ds(lo, source.shape[0])]
        copy = pltpu.make_async_copy(source, target, sems.at[len(started)])
        if rel is None:
            copy.start()
        else:
            pl.when(chosen(rel))(copy.start)
        started.append((copy, rel))
    def wait_for(kind):
        for (copy, rel), spec in zip(started, copies):
            if spec[2] != kind:
                continue
            if rel is None:
                copy.wait()
            else:
                pl.when(chosen(rel))(copy.wait)

    sources = (cells_ref,) + tuple(iter_refs)

    def plane_value(order, b, p):
        source = sources[order - 1]
        field = source[b, RADIUS + p]
        laplace = (3.0 * CENTER_COEF) * field
        for offset, weight in enumerate(STENCIL, 1):
            beside_all = source[b, RADIUS + p + offset] + source[b, RADIUS + p - offset]
            beside_all = beside_all + pltpu.roll(field, offset, 0) + pltpu.roll(field, ny - offset, 0)
            laplace = laplace + weight * beside_all
        laplace = laplace + zsum_ref[b, p]
        applied = -0.5 * laplace + pot_ref[(order - 1) * RADIUS + p] * field
        if order == 1:
            return (applied - SHIFT_C * field) / HALF_W
        before = sources[order - 2][b, 2 * RADIUS + p]
        return 2.0 * (applied - SHIFT_C * field) / HALF_W - before

    def along_z(order, planes):
        source = sources[order - 1]
        for b in range(block_orbs):
            rows = source[b, RADIUS : RADIUS + planes].reshape(planes * ny, nz)
            mixed = jnp.dot(rows, cz_ref[...], precision=lax.Precision.HIGHEST, preferred_element_type=jnp.float32)
            zsum_ref[b, :planes] = mixed.reshape(planes, ny, nz)

    wait_for("cells")
    along_z(1, slab + 2 * (DEG_MAX - 1) * RADIUS)
    wait_for("pot")
    for order in range(1, DEG_MAX):
        margin = (DEG_MAX - order) * RADIUS
        dest = iter_refs[order - 1]
        planes = slab + 2 * margin
        if order > 1:
            along_z(order, planes)
        for b in range(block_orbs):
            def body(p, carry, order=order, b=b, dest=dest):
                value = plane_value(order, b, p)
                plane = first + order * RADIUS + p
                keep = jnp.full((ny, nz), plane, jnp.int32)
                keep = (keep >= 0) & (keep < grid_planes)
                dest[b, p] = jnp.where(keep, value, 0.0)
                return carry
            lax.fori_loop(0, planes, body, 0, unroll=2)

    along_z(DEG_MAX, slab)
    for b in range(block_orbs):
        def last(p, carry, b=b):
            value = plane_value(DEG_MAX, b, p)
            levels = jnp.full((ny, nz), degree, jnp.int32)
            picked = iter_refs[0][b, (DEG_MAX - 1) * RADIUS + p]
            for order in range(2, DEG_MAX):
                picked = jnp.where(levels >= order, iter_refs[order - 1][b, (DEG_MAX - order) * RADIUS + p], picked)
            picked = jnp.where(levels >= DEG_MAX, value, picked)
            out_ref[b, p] = picked.astype(out_ref.dtype)
            return carry
        lax.fori_loop(0, slab, last, 0, unroll=2)


def chebyshev_filter(orbitals, potential, first, degree, grid_planes):
    block_orbs, slab, ny, nz = orbitals.shape
    reach = DEG_MAX * RADIUS
    operands, copies, zeros = halo_plan(orbitals, potential, reach, reach - RADIUS)
    smem = pl.BlockSpec(memory_space=pltpu.SMEM)
    hbm = pl.BlockSpec(memory_space=pl.ANY)
    vmem = pl.BlockSpec(memory_space=pltpu.VMEM)
    return pl.pallas_call(
        functools.partial(
            filter_kernel,
            copies=tuple(copies),
            zeros=tuple(zeros),
            n_in=len(operands),
            block_count=block_orbs,
            grid_planes=grid_planes,
        ),
        out_shape=jax.ShapeDtypeStruct((block_orbs, slab, ny, nz), jnp.bfloat16),
        in_specs=[smem, smem, vmem, hbm, hbm] + [vmem] * (len(operands) - 2),
        out_specs=vmem,
        scratch_shapes=[
            pltpu.VMEM((block_orbs, slab + 2 * reach, ny, nz), jnp.float32),
            pltpu.VMEM((slab + 2 * (reach - RADIUS), ny, nz), jnp.float32),
            pltpu.VMEM((block_orbs, slab + 2 * (reach - RADIUS), ny, nz), jnp.float32),
            pltpu.SemaphoreType.DMA((len(copies),)),
        ]
        + [
            pltpu.VMEM((block_orbs, slab + 2 * (DEG_MAX - order) * RADIUS, ny, nz), jnp.float32)
            for order in range(1, DEG_MAX)
        ],
    )(first, degree, jnp.asarray(circulant(nz)), *operands)


def inner_rows(left, right):
    return lax.dot_general(
        left, right, (((1,), (1,)), ((), ())), preferred_element_type=jnp.float32
    )


def per_device(orbitals, potential, degrees):
    block_orbs, slab = orbitals.shape[0], orbitals.shape[1]
    n_orb, n_dom = lax.axis_size("orb"), lax.axis_size("dom")
    grid_planes = slab * n_dom
    start = lax.axis_index("dom") * slab
    first = (start - DEG_MAX * RADIUS).astype(jnp.int32).reshape(1)
    filtered = chebyshev_filter(orbitals, potential, first, degrees.astype(jnp.int32), grid_planes)
    cell_count = orbitals.shape[1] * orbitals.shape[2] * orbitals.shape[3]
    total_cells = float(cell_count * n_dom)
    flattened = filtered.reshape(block_orbs, cell_count)
    mixed = lax.all_to_all(flattened, "orb", split_axis=1, concat_axis=0, tiled=True)
    partial_gram = inner_rows(mixed, mixed)
    rows = partial_gram.reshape(n_orb, 1, block_orbs, -1)
    sends = jnp.broadcast_to(rows, (n_orb, n_dom) + rows.shape[2:]).reshape((n_orb * n_dom,) + rows.shape[2:])
    gathered = lax.all_to_all(sends, ("orb", "dom"), split_axis=0, concat_axis=0, tiled=True)
    correlation = gathered.sum(axis=0) / total_cells
    return (filtered, correlation)


def solution(mesh):
    placed = (P("orb", "dom", None, None), P("dom", None, None), P("orb"))
    return jax.shard_map(
        per_device,
        mesh=mesh,
        in_specs=placed,
        out_specs=(P("orb", "dom", None, None), P("orb", None)),
        check_vma=False,
    )
```

```python
import functools

import numpy as np
import jax
import jax.numpy as jnp
from jax import lax
from jax.experimental import pallas as pl
from jax.experimental.pallas import tpu as pltpu
from jax.sharding import PartitionSpec as P

DEG_MAX = 3


CENTER_COEF = -5369.0 / 1800.0
STENCIL = (12.0 / 7.0, -15.0 / 56.0, 10.0 / 189.0, -1.0 / 112.0, 2.0 / 1925.0, -1.0 / 16632.0)
SHIFT_C = 8.5
HALF_W = 4.5
RADIUS = len(STENCIL)
FOLDED = tuple(-0.5 * weight / HALF_W for weight in STENCIL)
FOLDED_SHIFT = -SHIFT_C - 1.5 * CENTER_COEF


def circulant(n, scale):
    gap = (np.arange(n)[None, :] - np.arange(n)[:, None]) % n
    weights = np.zeros((n, n), np.float32)
    for offset, weight in enumerate(FOLDED, 1):
        weights[(gap == offset) | (gap == n - offset)] = np.float32(scale * np.float32(weight))
    return weights


def shifted(x, k):
    count = lax.axis_size("dom")
    pairs = [(i, i + k) for i in range(count) if 0 <= i + k < count]
    if not pairs:
        return jnp.zeros_like(x)
    return lax.ppermute(x, "dom", pairs)


def gather_plan(orbitals, potential, reach, pot_reach):
    block_orbs, slab = orbitals.shape[0], orbitals.shape[1]
    count = lax.axis_size("dom")
    packed = jnp.concatenate([orbitals, potential[None]], axis=0)
    operands = [orbitals, potential]
    copies = [(0, "all", "cells", reach, None), (1, "all", "pot", pot_reach, None)]
    zeros = []
    pairwise = count & (count - 1) == 0
    for k in range(1, count):
        source = [j ^ k if pairwise else (j - k) % count for j in range(count)]
        near = [j for j in range(count) if abs(source[j] - j) * slab <= pot_reach]
        far = [j for j in range(count) if j not in near]
        for group, values, with_pot in ((near, packed, True), (far, orbitals, False)):
            if not group:
                continue
            operands.append(lax.ppermute(values, "dom", [(source[j], j) for j in group]))
            for rel in sorted({source[j] - j for j in group}):
                devices = tuple(j for j in group if source[j] - j == rel)
                copies.append((len(operands) - 1, "orb" if with_pot else "all", "cells", reach + rel * slab, devices))
                if with_pot:
                    copies.append((len(operands) - 1, "pot", "pot", pot_reach + rel * slab, devices))
    for rel in range(-(reach // slab), reach // slab + 1):
        if rel != 0:
            zeros.append(("cells", reach + rel * slab, rel))
            if abs(rel) * slab <= pot_reach:
                zeros.append(("pot", pot_reach + rel * slab, rel))
    return operands, copies, zeros


def halo_plan(orbitals, potential, reach, pot_reach):
    block_orbs, slab = orbitals.shape[0], orbitals.shape[1]
    if reach % slab == 0 and pot_reach % slab == 0 and lax.axis_size("dom") - 1 <= reach // slab:
        return gather_plan(orbitals, potential, reach, pot_reach)
    operands = [orbitals, potential]
    copies = [(0, "all", "cells", reach, None), (1, "all", "pot", pot_reach, None)]
    packed = None
    k = 1
    while slab * (k - 1) < reach:
        count = min(slab, reach - slab * (k - 1))
        pot_count = max(0, min(slab, pot_reach - slab * (k - 1)))
        for sign in (1, -1):
            if pot_count == slab and count == slab:
                if packed is None:
                    packed = jnp.concatenate([orbitals, potential[None]], axis=0)
                parts = [(packed, "orb", count, "cells", reach), (None, "pot", count, "pot", pot_reach)]
            else:
                parts = [(orbitals, "all", count, "cells", reach)]
                if pot_count:
                    parts.append((potential, "all", pot_count, "pot", pot_reach))
            for values, part, size, dest, centre in parts:
                lo = centre - slab * (k - 1) - size if sign > 0 else centre + slab * k
                if values is not None:
                    axis = 0 if values is potential else 1
                    span = values.shape[axis]
                    if sign > 0:
                        piece = lax.slice_in_dim(values, span - size, span, axis=axis)
                    else:
                        piece = lax.slice_in_dim(values, 0, size, axis=axis)
                    operands.append(shifted(piece, sign * k))
                copies.append((len(operands) - 1, part, dest, lo, None))
        k += 1
    return operands, copies, []


def filter_kernel(first_ref, deg_ref, cz_ref, cz2_ref, *refs, copies, zeros, n_in, block_count, grid_planes):
    ins = refs[:n_in]
    out_ref = refs[n_in]
    cells_ref, pot_ref, potw_ref, zsum_ref, sems = refs[n_in + 1 : n_in + 6]
    iter_refs = refs[n_in + 6 :]
    block_orbs, _, ny, nz = cells_ref.shape
    slab = out_ref.shape[1]
    first = first_ref[0]
    degree = deg_ref[0]

    reach = DEG_MAX * RADIUS
    own_slab = (first + reach) // slab

    def inside(rel):
        return (own_slab + rel >= 0) & (own_slab + rel < grid_planes // slab)

    for dest, lo, rel in zeros:
        def clear(dest=dest, lo=lo):
            if dest == "cells":
                cells_ref[:, pl.ds(lo, slab)] = jnp.zeros((block_orbs, slab, ny, nz), jnp.float32)
            else:
                pot_ref[pl.ds(lo, slab)] = jnp.zeros((slab, ny, nz), jnp.float32)
        pl.when(jnp.logical_not(inside(rel)))(clear)
    def chosen(devices):
        hit = own_slab == devices[0]
        for device in devices[1:]:
            hit = hit | (own_slab == device)
        return hit

    started = []
    for index, part, dest, lo, rel in copies:
        source = ins[index]
        if part == "orb":
            source = source.at[pl.ds(0, block_count)]
        elif part == "pot":
            source = source.at[block_count]
        if dest == "cells":
            target = cells_ref.at[:, pl.ds(lo, source.shape[1])]
        else:
            target = pot_ref.at[pl.ds(lo, source.shape[0])]
        copy = pltpu.make_async_copy(source, target, sems.at[len(started)])
        if rel is None:
            copy.start()
        else:
            pl.when(chosen(rel))(copy.start)
        started.append((copy, rel))
    def wait_for(kind):
        for (copy, rel), spec in zip(started, copies):
            if spec[2] != kind:
                continue
            if rel is None:
                copy.wait()
            else:
                pl.when(chosen(rel))(copy.wait)

    sources = (cells_ref,) + tuple(iter_refs)

    def plane_value(order, b, p):
        source = sources[order - 1]
        scale = 1.0 if order == 1 else 2.0
        field = source[b, RADIUS + p]
        total = zsum_ref[b, p]
        for offset, weight in enumerate(FOLDED, 1):
            beside_all = source[b, RADIUS + p + offset] + source[b, RADIUS + p - offset]
            beside_all = beside_all + pltpu.roll(field, offset, 0) + pltpu.roll(field, ny - offset, 0)
            total = total + (scale * weight) * beside_all
        total = total + potw_ref[min(order, 2) - 1, (order - 1) * RADIUS + p] * field
        if order == 1:
            return total
        return total - sources[order - 2][b, 2 * RADIUS + p]

    def along_z(order, planes):
        source = sources[order - 1]
        weights = cz_ref if order == 1 else cz2_ref
        for b in range(block_orbs):
            rows = source[b, RADIUS : RADIUS + planes].reshape(planes * ny, nz)
            mixed = jnp.dot(rows, weights[...], precision=lax.Precision.HIGHEST, preferred_element_type=jnp.float32)
            zsum_ref[b, :planes] = mixed.reshape(planes, ny, nz)

    def coefficients(q, carry):
        coefficient = (pot_ref[q] + FOLDED_SHIFT) * (1.0 / HALF_W)
        potw_ref[0, q] = coefficient
        potw_ref[1, q] = coefficient + coefficient
        return carry

    wait_for("cells")
    along_z(1, slab + 2 * (DEG_MAX - 1) * RADIUS)
    wait_for("pot")
    lax.fori_loop(0, pot_ref.shape[0], coefficients, 0)
    for order in range(1, DEG_MAX):
        margin = (DEG_MAX - order) * RADIUS
        dest = iter_refs[order - 1]
        planes = slab + 2 * margin
        if order > 1:
            along_z(order, planes)
        first_plane = first + order * RADIUS
        lo = jnp.minimum(jnp.maximum(-first_plane, 0), planes)
        hi = jnp.maximum(jnp.minimum(grid_planes - first_plane, planes), lo)
        for b in range(block_orbs):
            def clear(p, carry, b=b, dest=dest):
                dest[b, p] = jnp.zeros((ny, nz), jnp.float32)
                return carry

            def pair(i, carry, order=order, b=b, dest=dest):
                p = lo + 2 * i
                dest[b, p] = plane_value(order, b, p)
                dest[b, p + 1] = plane_value(order, b, p + 1)
                return carry

            def tail(order=order, b=b, dest=dest):
                dest[b, hi - 1] = plane_value(order, b, hi - 1)

            lax.fori_loop(0, lo, clear, 0)
            lax.fori_loop(hi, planes, clear, 0)
            lax.fori_loop(0, (hi - lo) // 2, pair, 0)
            pl.when((hi - lo) % 2 == 1)(tail)

    along_z(DEG_MAX, slab)
    for b in range(block_orbs):
        def last(p, carry, b=b):
            value = plane_value(DEG_MAX, b, p)
            levels = jnp.full((ny, nz), degree, jnp.int32)
            picked = iter_refs[0][b, (DEG_MAX - 1) * RADIUS + p]
            for order in range(2, DEG_MAX):
                picked = jnp.where(levels >= order, iter_refs[order - 1][b, (DEG_MAX - order) * RADIUS + p], picked)
            picked = jnp.where(levels >= DEG_MAX, value, picked)
            out_ref[b, p] = picked.astype(out_ref.dtype)
            return carry
        lax.fori_loop(0, slab, last, 0, unroll=2)


def chebyshev_filter(orbitals, potential, first, degree, grid_planes):
    block_orbs, slab, ny, nz = orbitals.shape
    reach = DEG_MAX * RADIUS
    operands, copies, zeros = halo_plan(orbitals, potential, reach, reach - RADIUS)
    smem = pl.BlockSpec(memory_space=pltpu.SMEM)
    hbm = pl.BlockSpec(memory_space=pl.ANY)
    vmem = pl.BlockSpec(memory_space=pltpu.VMEM)
    return pl.pallas_call(
        functools.partial(
            filter_kernel,
            copies=tuple(copies),
            zeros=tuple(zeros),
            n_in=len(operands),
            block_count=block_orbs,
            grid_planes=grid_planes,
        ),
        out_shape=jax.ShapeDtypeStruct((block_orbs, slab, ny, nz), jnp.bfloat16),
        in_specs=[smem, smem, vmem, vmem, hbm, hbm] + [vmem] * (len(operands) - 2),
        out_specs=vmem,
        scratch_shapes=[
            pltpu.VMEM((block_orbs, slab + 2 * reach, ny, nz), jnp.float32),
            pltpu.VMEM((slab + 2 * (reach - RADIUS), ny, nz), jnp.float32),
            pltpu.VMEM((2, slab + 2 * (reach - RADIUS), ny, nz), jnp.float32),
            pltpu.VMEM((block_orbs, slab + 2 * (reach - RADIUS), ny, nz), jnp.float32),
            pltpu.SemaphoreType.DMA((len(copies),)),
        ]
        + [
            pltpu.VMEM((block_orbs, slab + 2 * (DEG_MAX - order) * RADIUS, ny, nz), jnp.float32)
            for order in range(1, DEG_MAX)
        ],
    )(first, degree, jnp.asarray(circulant(nz, 1.0)), jnp.asarray(circulant(nz, 2.0)), *operands)


def inner_rows(left, right):
    return lax.dot_general(
        left, right, (((1,), (1,)), ((), ())), preferred_element_type=jnp.float32
    )


def per_device(orbitals, potential, degrees):
    block_orbs, slab = orbitals.shape[0], orbitals.shape[1]
    n_orb, n_dom = lax.axis_size("orb"), lax.axis_size("dom")
    grid_planes = slab * n_dom
    start = lax.axis_index("dom") * slab
    first = (start - DEG_MAX * RADIUS).astype(jnp.int32).reshape(1)
    filtered = chebyshev_filter(orbitals, potential, first, degrees.astype(jnp.int32), grid_planes)
    cell_count = orbitals.shape[1] * orbitals.shape[2] * orbitals.shape[3]
    total_cells = float(cell_count * n_dom)
    flattened = filtered.reshape(block_orbs, cell_count)
    mixed = lax.all_to_all(flattened, "orb", split_axis=1, concat_axis=0, tiled=True)
    partial_gram = inner_rows(mixed, mixed)
    rows = partial_gram.reshape(n_orb, 1, block_orbs, -1)
    sends = jnp.broadcast_to(rows, (n_orb, n_dom) + rows.shape[2:]).reshape((n_orb * n_dom,) + rows.shape[2:])
    gathered = lax.all_to_all(sends, ("orb", "dom"), split_axis=0, concat_axis=0, tiled=True)
    correlation = gathered.sum(axis=0) / total_cells
    return (filtered, correlation)


def solution(mesh):
    placed = (P("orb", "dom", None, None), P("dom", None, None), P("orb"))
    return jax.shard_map(
        per_device,
        mesh=mesh,
        in_specs=placed,
        out_specs=(P("orb", "dom", None, None), P("orb", None)),
        check_vma=False,
    )
```

```python
import functools

import numpy as np
import jax
import jax.numpy as jnp
from jax import lax
from jax.experimental import pallas as pl
from jax.experimental.pallas import tpu as pltpu
from jax.sharding import PartitionSpec as P

DEG_MAX = 3


CENTER_COEF = -5369.0 / 1800.0
STENCIL = (12.0 / 7.0, -15.0 / 56.0, 10.0 / 189.0, -1.0 / 112.0, 2.0 / 1925.0, -1.0 / 16632.0)
SHIFT_C = 8.5
HALF_W = 4.5
RADIUS = len(STENCIL)
STEP = 6
FOLDED = tuple(-0.5 * weight / HALF_W for weight in STENCIL)
FOLDED_SHIFT = -SHIFT_C - 1.5 * CENTER_COEF


def circulant(n, scale):
    gap = (np.arange(n)[None, :] - np.arange(n)[:, None]) % n
    weights = np.zeros((n, n), np.float32)
    for offset, weight in enumerate(FOLDED, 1):
        weights[(gap == offset) | (gap == n - offset)] = np.float32(scale * np.float32(weight))
    return weights


def shifted(x, k):
    count = lax.axis_size("dom")
    pairs = [(i, i + k) for i in range(count) if 0 <= i + k < count]
    if not pairs:
        return jnp.zeros_like(x)
    return lax.ppermute(x, "dom", pairs)


def gather_plan(orbitals, potential, reach, pot_reach):
    block_orbs, slab = orbitals.shape[0], orbitals.shape[1]
    count = lax.axis_size("dom")
    packed = jnp.concatenate([orbitals, potential[None]], axis=0)
    operands = [orbitals, potential]
    copies = [(0, "all", "cells", reach, None), (1, "all", "pot", pot_reach, None)]
    zeros = []
    pairwise = count & (count - 1) == 0
    for k in range(1, count):
        source = [j ^ k if pairwise else (j - k) % count for j in range(count)]
        near = [j for j in range(count) if abs(source[j] - j) * slab <= pot_reach]
        far = [j for j in range(count) if j not in near]
        for group, values, with_pot in ((near, packed, True), (far, orbitals, False)):
            if not group:
                continue
            operands.append(lax.ppermute(values, "dom", [(source[j], j) for j in group]))
            for rel in sorted({source[j] - j for j in group}):
                devices = tuple(j for j in group if source[j] - j == rel)
                copies.append((len(operands) - 1, "orb" if with_pot else "all", "cells", reach + rel * slab, devices))
                if with_pot:
                    copies.append((len(operands) - 1, "pot", "pot", pot_reach + rel * slab, devices))
    for rel in range(-(reach // slab), reach // slab + 1):
        if rel != 0:
            zeros.append(("cells", reach + rel * slab, rel))
            if abs(rel) * slab <= pot_reach:
                zeros.append(("pot", pot_reach + rel * slab, rel))
    return operands, copies, zeros


def halo_plan(orbitals, potential, reach, pot_reach):
    block_orbs, slab = orbitals.shape[0], orbitals.shape[1]
    if reach % slab == 0 and pot_reach % slab == 0 and lax.axis_size("dom") - 1 <= reach // slab:
        return gather_plan(orbitals, potential, reach, pot_reach)
    operands = [orbitals, potential]
    copies = [(0, "all", "cells", reach, None), (1, "all", "pot", pot_reach, None)]
    packed = None
    k = 1
    while slab * (k - 1) < reach:
        count = min(slab, reach - slab * (k - 1))
        pot_count = max(0, min(slab, pot_reach - slab * (k - 1)))
        for sign in (1, -1):
            if pot_count == slab and count == slab:
                if packed is None:
                    packed = jnp.concatenate([orbitals, potential[None]], axis=0)
                parts = [(packed, "orb", count, "cells", reach), (None, "pot", count, "pot", pot_reach)]
            else:
                parts = [(orbitals, "all", count, "cells", reach)]
                if pot_count:
                    parts.append((potential, "all", pot_count, "pot", pot_reach))
            for values, part, size, dest, centre in parts:
                lo = centre - slab * (k - 1) - size if sign > 0 else centre + slab * k
                if values is not None:
                    axis = 0 if values is potential else 1
                    span = values.shape[axis]
                    if sign > 0:
                        piece = lax.slice_in_dim(values, span - size, span, axis=axis)
                    else:
                        piece = lax.slice_in_dim(values, 0, size, axis=axis)
                    operands.append(shifted(piece, sign * k))
                copies.append((len(operands) - 1, part, dest, lo, None))
        k += 1
    return operands, copies, []


def filter_kernel(first_ref, deg_ref, cz_ref, cz2_ref, *refs, copies, zeros, n_in, block_count, grid_planes):
    ins = refs[:n_in]
    out_ref = refs[n_in]
    cells_ref, pot_ref, potw_ref, zsum_ref, sems = refs[n_in + 1 : n_in + 6]
    iter_refs = refs[n_in + 6 :]
    block_orbs, _, ny, nz = cells_ref.shape
    slab = out_ref.shape[1]
    first = first_ref[0]
    degree = deg_ref[0]

    reach = DEG_MAX * RADIUS
    own_slab = (first + reach) // slab

    def inside(rel):
        return (own_slab + rel >= 0) & (own_slab + rel < grid_planes // slab)

    for dest, lo, rel in zeros:
        def clear(dest=dest, lo=lo):
            if dest == "cells":
                cells_ref[:, pl.ds(lo, slab)] = jnp.zeros((block_orbs, slab, ny, nz), jnp.float32)
            else:
                pot_ref[pl.ds(lo, slab)] = jnp.zeros((slab, ny, nz), jnp.float32)
        pl.when(jnp.logical_not(inside(rel)))(clear)
    def chosen(devices):
        hit = own_slab == devices[0]
        for device in devices[1:]:
            hit = hit | (own_slab == device)
        return hit

    started = []
    for index, part, dest, lo, rel in copies:
        source = ins[index]
        if part == "orb":
            source = source.at[pl.ds(0, block_count)]
        elif part == "pot":
            source = source.at[block_count]
        if dest == "cells":
            target = cells_ref.at[:, pl.ds(lo, source.shape[1])]
        else:
            target = pot_ref.at[pl.ds(lo, source.shape[0])]
        copy = pltpu.make_async_copy(source, target, sems.at[len(started)])
        if rel is None:
            copy.start()
        else:
            pl.when(chosen(rel))(copy.start)
        started.append((copy, rel))
    def wait_for(kind):
        for (copy, rel), spec in zip(started, copies):
            if spec[2] != kind:
                continue
            if rel is None:
                copy.wait()
            else:
                pl.when(chosen(rel))(copy.wait)

    sources = (cells_ref,) + tuple(iter_refs)

    def plane_value(order, b, p):
        source = sources[order - 1]
        scale = 1.0 if order == 1 else 2.0
        field = source[b, RADIUS + p]
        total = zsum_ref[b, p]
        for offset, weight in enumerate(FOLDED, 1):
            beside_all = source[b, RADIUS + p + offset] + source[b, RADIUS + p - offset]
            beside_all = beside_all + pltpu.roll(field, offset, 0) + pltpu.roll(field, ny - offset, 0)
            total = total + (scale * weight) * beside_all
        total = total + potw_ref[min(order, 2) - 1, (order - 1) * RADIUS + p] * field
        if order == 1:
            return total
        return total - sources[order - 2][b, 2 * RADIUS + p]

    def along_z(order, planes):
        source = sources[order - 1]
        weights = cz_ref if order == 1 else cz2_ref
        for b in range(block_orbs):
            rows = source[b, RADIUS : RADIUS + planes].reshape(planes * ny, nz)
            mixed = jnp.dot(rows, weights[...], precision=lax.Precision.HIGHEST, preferred_element_type=jnp.float32)
            zsum_ref[b, :planes] = mixed.reshape(planes, ny, nz)

    def coefficients(q, carry):
        coefficient = (pot_ref[q] + FOLDED_SHIFT) * (1.0 / HALF_W)
        potw_ref[0, q] = coefficient
        potw_ref[1, q] = coefficient + coefficient
        return carry

    wait_for("cells")
    along_z(1, slab + 2 * (DEG_MAX - 1) * RADIUS)
    wait_for("pot")
    lax.fori_loop(0, pot_ref.shape[0], coefficients, 0)
    for order in range(1, DEG_MAX):
        margin = (DEG_MAX - order) * RADIUS
        dest = iter_refs[order - 1]
        planes = slab + 2 * margin
        if order > 1:
            along_z(order, planes)
        first_plane = first + order * RADIUS
        lo = jnp.minimum(jnp.maximum(-first_plane, 0), planes)
        hi = jnp.maximum(jnp.minimum(grid_planes - first_plane, planes), lo)
        for b in range(block_orbs):
            def clear(p, carry, b=b, dest=dest):
                dest[b, p] = jnp.zeros((ny, nz), jnp.float32)
                return carry

            def group(i, carry, order=order, b=b, dest=dest):
                for j in range(STEP):
                    dest[b, lo + STEP * i + j] = plane_value(order, b, lo + STEP * i + j)
                return carry

            def single(p, carry, order=order, b=b, dest=dest):
                dest[b, p] = plane_value(order, b, p)
                return carry

            lax.fori_loop(0, lo, clear, 0)
            lax.fori_loop(hi, planes, clear, 0)
            lax.fori_loop(0, (hi - lo) // STEP, group, 0)
            lax.fori_loop(lo + STEP * ((hi - lo) // STEP), hi, single, 0)

    along_z(DEG_MAX, slab)
    for b in range(block_orbs):
        def last(p, carry, b=b):
            value = plane_value(DEG_MAX, b, p)
            levels = jnp.full((ny, nz), degree, jnp.int32)
            picked = iter_refs[0][b, (DEG_MAX - 1) * RADIUS + p]
            for order in range(2, DEG_MAX):
                picked = jnp.where(levels >= order, iter_refs[order - 1][b, (DEG_MAX - order) * RADIUS + p], picked)
            picked = jnp.where(levels >= DEG_MAX, value, picked)
            out_ref[b, p] = picked.astype(out_ref.dtype)
            return carry
        lax.fori_loop(0, slab, last, 0, unroll=2)


def chebyshev_filter(orbitals, potential, first, degree, grid_planes):
    block_orbs, slab, ny, nz = orbitals.shape
    reach = DEG_MAX * RADIUS
    operands, copies, zeros = halo_plan(orbitals, potential, reach, reach - RADIUS)
    smem = pl.BlockSpec(memory_space=pltpu.SMEM)
    hbm = pl.BlockSpec(memory_space=pl.ANY)
    vmem = pl.BlockSpec(memory_space=pltpu.VMEM)
    return pl.pallas_call(
        functools.partial(
            filter_kernel,
            copies=tuple(copies),
            zeros=tuple(zeros),
            n_in=len(operands),
            block_count=block_orbs,
            grid_planes=grid_planes,
        ),
        out_shape=jax.ShapeDtypeStruct((block_orbs, slab, ny, nz), jnp.bfloat16),
        in_specs=[smem, smem, vmem, vmem, hbm, hbm] + [vmem] * (len(operands) - 2),
        out_specs=vmem,
        scratch_shapes=[
            pltpu.VMEM((block_orbs, slab + 2 * reach, ny, nz), jnp.float32),
            pltpu.VMEM((slab + 2 * (reach - RADIUS), ny, nz), jnp.float32),
            pltpu.VMEM((2, slab + 2 * (reach - RADIUS), ny, nz), jnp.float32),
            pltpu.VMEM((block_orbs, slab + 2 * (reach - RADIUS), ny, nz), jnp.float32),
            pltpu.SemaphoreType.DMA((len(copies),)),
        ]
        + [
            pltpu.VMEM((block_orbs, slab + 2 * (DEG_MAX - order) * RADIUS, ny, nz), jnp.float32)
            for order in range(1, DEG_MAX)
        ],
    )(first, degree, jnp.asarray(circulant(nz, 1.0)), jnp.asarray(circulant(nz, 2.0)), *operands)


def inner_rows(left, right):
    return lax.dot_general(
        left, right, (((1,), (1,)), ((), ())), preferred_element_type=jnp.float32
    )


def per_device(orbitals, potential, degrees):
    block_orbs, slab = orbitals.shape[0], orbitals.shape[1]
    n_orb, n_dom = lax.axis_size("orb"), lax.axis_size("dom")
    grid_planes = slab * n_dom
    start = lax.axis_index("dom") * slab
    first = (start - DEG_MAX * RADIUS).astype(jnp.int32).reshape(1)
    filtered = chebyshev_filter(orbitals, potential, first, degrees.astype(jnp.int32), grid_planes)
    cell_count = orbitals.shape[1] * orbitals.shape[2] * orbitals.shape[3]
    total_cells = float(cell_count * n_dom)
    flattened = filtered.reshape(block_orbs, cell_count)
    mixed = lax.all_to_all(flattened, "orb", split_axis=1, concat_axis=0, tiled=True)
    partial_gram = inner_rows(mixed, mixed) / total_cells
    rows = partial_gram.reshape(n_orb, 1, block_orbs, -1)
    sends = jnp.broadcast_to(rows, (n_orb, n_dom) + rows.shape[2:]).reshape((n_orb * n_dom,) + rows.shape[2:])
    gathered = lax.all_to_all(sends, ("orb", "dom"), split_axis=0, concat_axis=0, tiled=True)
    correlation = gathered.sum(axis=0)
    return (filtered, correlation)


def solution(mesh):
    placed = (P("orb", "dom", None, None), P("dom", None, None), P("orb"))
    return jax.shard_map(
        per_device,
        mesh=mesh,
        in_specs=placed,
        out_specs=(P("orb", "dom", None, None), P("orb", None)),
        check_vma=False,
    )
```

```python
import functools

import numpy as np
import jax
import jax.numpy as jnp
from jax import lax
from jax.experimental import pallas as pl
from jax.experimental.pallas import tpu as pltpu
from jax.sharding import PartitionSpec as P

DEG_MAX = 3


CENTER_COEF = -5369.0 / 1800.0
STENCIL = (12.0 / 7.0, -15.0 / 56.0, 10.0 / 189.0, -1.0 / 112.0, 2.0 / 1925.0, -1.0 / 16632.0)
SHIFT_C = 8.5
HALF_W = 4.5
RADIUS = len(STENCIL)
STEP = 6
FOLDED = tuple(-0.5 * weight / HALF_W for weight in STENCIL)
FOLDED_SHIFT = -SHIFT_C - 1.5 * CENTER_COEF


def circulant(n, scale):
    gap = (np.arange(n)[None, :] - np.arange(n)[:, None]) % n
    weights = np.zeros((n, n), np.float32)
    for offset, weight in enumerate(FOLDED, 1):
        weights[(gap == offset) | (gap == n - offset)] = np.float32(scale * np.float32(weight))
    return weights


def shifted(x, k):
    count = lax.axis_size("dom")
    pairs = [(i, i + k) for i in range(count) if 0 <= i + k < count]
    if not pairs:
        return jnp.zeros_like(x)
    return lax.ppermute(x, "dom", pairs)


def gather_plan(orbitals, potential, reach, pot_reach):
    block_orbs, slab = orbitals.shape[0], orbitals.shape[1]
    count = lax.axis_size("dom")
    packed = jnp.concatenate([orbitals, potential[None]], axis=0)
    operands = [orbitals, potential]
    copies = [(0, "all", "cells", reach, None), (1, "all", "pot", pot_reach, None)]
    zeros = []
    pairwise = count & (count - 1) == 0
    for k in reversed(range(1, count)):
        source = [j ^ k if pairwise else (j - k) % count for j in range(count)]
        near = [j for j in range(count) if abs(source[j] - j) * slab <= pot_reach]
        far = [j for j in range(count) if j not in near]
        for group, values, with_pot in ((near, packed, True), (far, orbitals, False)):
            if not group:
                continue
            operands.append(lax.ppermute(values, "dom", [(source[j], j) for j in group]))
            for rel in sorted({source[j] - j for j in group}):
                devices = tuple(j for j in group if source[j] - j == rel)
                copies.append((len(operands) - 1, "orb" if with_pot else "all", "cells", reach + rel * slab, devices))
                if with_pot:
                    copies.append((len(operands) - 1, "pot", "pot", pot_reach + rel * slab, devices))
    for rel in range(-(reach // slab), reach // slab + 1):
        if rel != 0:
            zeros.append(("cells", reach + rel * slab, rel))
            if abs(rel) * slab <= pot_reach:
                zeros.append(("pot", pot_reach + rel * slab, rel))
    return operands, copies, zeros


def halo_plan(orbitals, potential, reach, pot_reach):
    block_orbs, slab = orbitals.shape[0], orbitals.shape[1]
    if reach % slab == 0 and pot_reach % slab == 0 and lax.axis_size("dom") - 1 <= reach // slab:
        return gather_plan(orbitals, potential, reach, pot_reach)
    operands = [orbitals, potential]
    copies = [(0, "all", "cells", reach, None), (1, "all", "pot", pot_reach, None)]
    packed = None
    k = 1
    while slab * (k - 1) < reach:
        count = min(slab, reach - slab * (k - 1))
        pot_count = max(0, min(slab, pot_reach - slab * (k - 1)))
        for sign in (1, -1):
            if pot_count == slab and count == slab:
                if packed is None:
                    packed = jnp.concatenate([orbitals, potential[None]], axis=0)
                parts = [(packed, "orb", count, "cells", reach), (None, "pot", count, "pot", pot_reach)]
            else:
                parts = [(orbitals, "all", count, "cells", reach)]
                if pot_count:
                    parts.append((potential, "all", pot_count, "pot", pot_reach))
            for values, part, size, dest, centre in parts:
                lo = centre - slab * (k - 1) - size if sign > 0 else centre + slab * k
                if values is not None:
                    axis = 0 if values is potential else 1
                    span = values.shape[axis]
                    if sign > 0:
                        piece = lax.slice_in_dim(values, span - size, span, axis=axis)
                    else:
                        piece = lax.slice_in_dim(values, 0, size, axis=axis)
                    operands.append(shifted(piece, sign * k))
                copies.append((len(operands) - 1, part, dest, lo, None))
        k += 1
    return operands, copies, []


def filter_kernel(first_ref, deg_ref, cz_ref, cz2_ref, *refs, copies, zeros, n_in, block_count, grid_planes):
    ins = refs[:n_in]
    out_ref = refs[n_in]
    cells_ref, pot_ref, potw_ref, zsum_ref, sems = refs[n_in + 1 : n_in + 6]
    iter_refs = refs[n_in + 6 :]
    block_orbs, _, ny, nz = cells_ref.shape
    slab = out_ref.shape[1]
    first = first_ref[0]
    degree = deg_ref[0]

    reach = DEG_MAX * RADIUS
    own_slab = (first + reach) // slab

    def inside(rel):
        return (own_slab + rel >= 0) & (own_slab + rel < grid_planes // slab)

    for dest, lo, rel in zeros:
        def clear(dest=dest, lo=lo):
            if dest == "cells":
                cells_ref[:, pl.ds(lo, slab)] = jnp.zeros((block_orbs, slab, ny, nz), jnp.float32)
            else:
                pot_ref[pl.ds(lo, slab)] = jnp.zeros((slab, ny, nz), jnp.float32)
        pl.when(jnp.logical_not(inside(rel)))(clear)
    def chosen(devices):
        hit = own_slab == devices[0]
        for device in devices[1:]:
            hit = hit | (own_slab == device)
        return hit

    started = []
    for index, part, dest, lo, rel in copies:
        source = ins[index]
        if part == "orb":
            source = source.at[pl.ds(0, block_count)]
        elif part == "pot":
            source = source.at[block_count]
        if dest == "cells":
            target = cells_ref.at[:, pl.ds(lo, source.shape[1])]
        else:
            target = pot_ref.at[pl.ds(lo, source.shape[0])]
        copy = pltpu.make_async_copy(source, target, sems.at[len(started)])
        if rel is None:
            copy.start()
        else:
            pl.when(chosen(rel))(copy.start)
        started.append((copy, rel))
    def wait_for(kind):
        for (copy, rel), spec in zip(started, copies):
            if spec[2] != kind:
                continue
            if rel is None:
                copy.wait()
            else:
                pl.when(chosen(rel))(copy.wait)

    sources = (cells_ref,) + tuple(iter_refs)

    def plane_value(order, b, p):
        source = sources[order - 1]
        scale = 1.0 if order == 1 else 2.0
        field = source[b, RADIUS + p]
        total = zsum_ref[b, p]
        for offset, weight in enumerate(FOLDED, 1):
            beside_all = source[b, RADIUS + p + offset] + source[b, RADIUS + p - offset]
            beside_all = beside_all + pltpu.roll(field, offset, 0) + pltpu.roll(field, ny - offset, 0)
            total = total + (scale * weight) * beside_all
        total = total + potw_ref[min(order, 2) - 1, (order - 1) * RADIUS + p] * field
        if order == 1:
            return total
        return total - sources[order - 2][b, 2 * RADIUS + p]

    def along_z(order, planes):
        source = sources[order - 1]
        weights = cz_ref if order == 1 else cz2_ref
        for b in range(block_orbs):
            rows = source[b, RADIUS : RADIUS + planes].reshape(planes * ny, nz)
            mixed = jnp.dot(rows, weights[...], precision=lax.Precision.HIGHEST, preferred_element_type=jnp.float32)
            zsum_ref[b, :planes] = mixed.reshape(planes, ny, nz)

    def coefficients(q, carry):
        coefficient = (pot_ref[q] + FOLDED_SHIFT) * (1.0 / HALF_W)
        potw_ref[0, q] = coefficient
        potw_ref[1, q] = coefficient + coefficient
        return carry

    wait_for("cells")
    along_z(1, slab + 2 * (DEG_MAX - 1) * RADIUS)
    wait_for("pot")
    lax.fori_loop(0, pot_ref.shape[0], coefficients, 0)
    for order in range(1, DEG_MAX):
        margin = (DEG_MAX - order) * RADIUS
        dest = iter_refs[order - 1]
        planes = slab + 2 * margin
        if order > 1:
            along_z(order, planes)
        first_plane = first + order * RADIUS
        lo = jnp.minimum(jnp.maximum(-first_plane, 0), planes)
        hi = jnp.maximum(jnp.minimum(grid_planes - first_plane, planes), lo)
        for b in range(block_orbs):
            def clear(p, carry, b=b, dest=dest):
                dest[b, p] = jnp.zeros((ny, nz), jnp.float32)
                return carry

            def group(i, carry, order=order, b=b, dest=dest):
                for j in range(STEP):
                    dest[b, lo + STEP * i + j] = plane_value(order, b, lo + STEP * i + j)
                return carry

            def single(p, carry, order=order, b=b, dest=dest):
                dest[b, p] = plane_value(order, b, p)
                return carry

            lax.fori_loop(0, lo, clear, 0)
            lax.fori_loop(hi, planes, clear, 0)
            lax.fori_loop(0, (hi - lo) // STEP, group, 0)
            lax.fori_loop(lo + STEP * ((hi - lo) // STEP), hi, single, 0)

    along_z(DEG_MAX, slab)
    for b in range(block_orbs):
        def last(p, carry, b=b):
            value = plane_value(DEG_MAX, b, p)
            levels = jnp.full((ny, nz), degree, jnp.int32)
            picked = iter_refs[0][b, (DEG_MAX - 1) * RADIUS + p]
            for order in range(2, DEG_MAX):
                picked = jnp.where(levels >= order, iter_refs[order - 1][b, (DEG_MAX - order) * RADIUS + p], picked)
            picked = jnp.where(levels >= DEG_MAX, value, picked)
            out_ref[b, p] = picked.astype(out_ref.dtype)
            return carry
        lax.fori_loop(0, slab, last, 0, unroll=2)


def chebyshev_filter(orbitals, potential, first, degree, grid_planes):
    block_orbs, slab, ny, nz = orbitals.shape
    reach = DEG_MAX * RADIUS
    operands, copies, zeros = halo_plan(orbitals, potential, reach, reach - RADIUS)
    smem = pl.BlockSpec(memory_space=pltpu.SMEM)
    hbm = pl.BlockSpec(memory_space=pl.ANY)
    vmem = pl.BlockSpec(memory_space=pltpu.VMEM)
    return pl.pallas_call(
        functools.partial(
            filter_kernel,
            copies=tuple(copies),
            zeros=tuple(zeros),
            n_in=len(operands),
            block_count=block_orbs,
            grid_planes=grid_planes,
        ),
        out_shape=jax.ShapeDtypeStruct((block_orbs, slab, ny, nz), jnp.bfloat16),
        in_specs=[smem, smem, vmem, vmem, hbm, hbm] + [vmem] * (len(operands) - 2),
        out_specs=vmem,
        scratch_shapes=[
            pltpu.VMEM((block_orbs, slab + 2 * reach, ny, nz), jnp.float32),
            pltpu.VMEM((slab + 2 * (reach - RADIUS), ny, nz), jnp.float32),
            pltpu.VMEM((2, slab + 2 * (reach - RADIUS), ny, nz), jnp.float32),
            pltpu.VMEM((block_orbs, slab + 2 * (reach - RADIUS), ny, nz), jnp.float32),
            pltpu.SemaphoreType.DMA((len(copies),)),
        ]
        + [
            pltpu.VMEM((block_orbs, slab + 2 * (DEG_MAX - order) * RADIUS, ny, nz), jnp.float32)
            for order in range(1, DEG_MAX)
        ],
    )(first, degree, jnp.asarray(circulant(nz, 1.0)), jnp.asarray(circulant(nz, 2.0)), *operands)


def inner_rows(left, right):
    return lax.dot_general(
        left, right, (((1,), (1,)), ((), ())), preferred_element_type=jnp.float32
    )


def per_device(orbitals, potential, degrees):
    block_orbs, slab = orbitals.shape[0], orbitals.shape[1]
    n_orb, n_dom = lax.axis_size("orb"), lax.axis_size("dom")
    grid_planes = slab * n_dom
    start = lax.axis_index("dom") * slab
    first = (start - DEG_MAX * RADIUS).astype(jnp.int32).reshape(1)
    filtered = chebyshev_filter(orbitals, potential, first, degrees.astype(jnp.int32), grid_planes)
    cell_count = orbitals.shape[1] * orbitals.shape[2] * orbitals.shape[3]
    total_cells = float(cell_count * n_dom)
    flattened = filtered.reshape(block_orbs, cell_count)
    mixed = lax.all_to_all(flattened, "orb", split_axis=1, concat_axis=0, tiled=True)
    partial_gram = inner_rows(mixed, mixed) / total_cells
    rows = partial_gram.reshape(n_orb, 1, block_orbs, -1)
    sends = jnp.broadcast_to(rows, (n_orb, n_dom) + rows.shape[2:]).reshape((n_orb * n_dom,) + rows.shape[2:])
    gathered = lax.all_to_all(sends, ("orb", "dom"), split_axis=0, concat_axis=0, tiled=True)
    correlation = gathered.sum(axis=0)
    return (filtered, correlation)


def solution(mesh):
    placed = (P("orb", "dom", None, None), P("dom", None, None), P("orb"))
    return jax.shard_map(
        per_device,
        mesh=mesh,
        in_specs=placed,
        out_specs=(P("orb", "dom", None, None), P("orb", None)),
        check_vma=False,
    )
```

```python
import functools

import numpy as np
import jax
import jax.numpy as jnp
from jax import lax
from jax.experimental import pallas as pl
from jax.experimental.pallas import tpu as pltpu
from jax.sharding import PartitionSpec as P

DEG_MAX = 3


CENTER_COEF = -5369.0 / 1800.0
STENCIL = (12.0 / 7.0, -15.0 / 56.0, 10.0 / 189.0, -1.0 / 112.0, 2.0 / 1925.0, -1.0 / 16632.0)
SHIFT_C = 8.5
HALF_W = 4.5
RADIUS = len(STENCIL)
STEP = 6
FOLDED = tuple(-0.5 * weight / HALF_W for weight in STENCIL)
FOLDED_SHIFT = -SHIFT_C - 1.5 * CENTER_COEF


def circulant(n, scale):
    gap = (np.arange(n)[None, :] - np.arange(n)[:, None]) % n
    weights = np.zeros((n, n), np.float32)
    for offset, weight in enumerate(FOLDED, 1):
        weights[(gap == offset) | (gap == n - offset)] = np.float32(scale * np.float32(weight))
    return weights


def shifted(x, k):
    count = lax.axis_size("dom")
    pairs = [(i, i + k) for i in range(count) if 0 <= i + k < count]
    if not pairs:
        return jnp.zeros_like(x)
    return lax.ppermute(x, "dom", pairs)


def gather_plan(orbitals, potential, reach, pot_reach):
    block_orbs, slab = orbitals.shape[0], orbitals.shape[1]
    count = lax.axis_size("dom")
    packed = jnp.concatenate([orbitals, potential[None]], axis=0)
    operands = [orbitals, potential]
    copies = [(0, "all", "cells", reach, None), (1, "all", "pot", pot_reach, None)]
    zeros = []
    pairwise = count & (count - 1) == 0
    for k in range(1, count):
        source = [j ^ k if pairwise else (j - k) % count for j in range(count)]
        near = [j for j in range(count) if abs(source[j] - j) * slab <= pot_reach]
        far = [j for j in range(count) if j not in near]
        for group, values, with_pot in ((near, packed, True), (far, orbitals, False)):
            if not group:
                continue
            operands.append(lax.ppermute(values, "dom", [(source[j], j) for j in group]))
            for rel in sorted({source[j] - j for j in group}):
                devices = tuple(j for j in group if source[j] - j == rel)
                copies.append((len(operands) - 1, "orb" if with_pot else "all", "cells", reach + rel * slab, devices))
                if with_pot:
                    copies.append((len(operands) - 1, "pot", "pot", pot_reach + rel * slab, devices))
    for rel in range(-(reach // slab), reach // slab + 1):
        if rel != 0:
            zeros.append(("cells", reach + rel * slab, rel))
            if abs(rel) * slab <= pot_reach:
                zeros.append(("pot", pot_reach + rel * slab, rel))
    return operands, copies, zeros


def halo_plan(orbitals, potential, reach, pot_reach):
    block_orbs, slab = orbitals.shape[0], orbitals.shape[1]
    if reach % slab == 0 and pot_reach % slab == 0 and lax.axis_size("dom") - 1 <= reach // slab:
        return gather_plan(orbitals, potential, reach, pot_reach)
    operands = [orbitals, potential]
    copies = [(0, "all", "cells", reach, None), (1, "all", "pot", pot_reach, None)]
    packed = None
    k = 1
    while slab * (k - 1) < reach:
        count = min(slab, reach - slab * (k - 1))
        pot_count = max(0, min(slab, pot_reach - slab * (k - 1)))
        for sign in (1, -1):
            if pot_count == slab and count == slab:
                if packed is None:
                    packed = jnp.concatenate([orbitals, potential[None]], axis=0)
                parts = [(packed, "orb", count, "cells", reach), (None, "pot", count, "pot", pot_reach)]
            else:
                parts = [(orbitals, "all", count, "cells", reach)]
                if pot_count:
                    parts.append((potential, "all", pot_count, "pot", pot_reach))
            for values, part, size, dest, centre in parts:
                lo = centre - slab * (k - 1) - size if sign > 0 else centre + slab * k
                if values is not None:
                    axis = 0 if values is potential else 1
                    span = values.shape[axis]
                    if sign > 0:
                        piece = lax.slice_in_dim(values, span - size, span, axis=axis)
                    else:
                        piece = lax.slice_in_dim(values, 0, size, axis=axis)
                    operands.append(shifted(piece, sign * k))
                copies.append((len(operands) - 1, part, dest, lo, None))
        k += 1
    return operands, copies, []


def filter_kernel(first_ref, deg_ref, cz_ref, cz2_ref, *refs, copies, zeros, n_in, block_count, grid_planes):
    ins = refs[:n_in]
    out_ref = refs[n_in]
    cells_ref, pot_ref, potw_ref, zsum_ref, sems = refs[n_in + 1 : n_in + 6]
    iter_refs = refs[n_in + 6 :]
    block_orbs, _, ny, nz = cells_ref.shape
    slab = out_ref.shape[1]
    first = first_ref[0]
    degree = deg_ref[0]

    reach = DEG_MAX * RADIUS
    own_slab = (first + reach) // slab

    def inside(rel):
        return (own_slab + rel >= 0) & (own_slab + rel < grid_planes // slab)

    for dest, lo, rel in zeros:
        def clear(dest=dest, lo=lo):
            if dest == "cells":
                cells_ref[:, pl.ds(lo, slab)] = jnp.zeros((block_orbs, slab, ny, nz), jnp.float32)
            else:
                pot_ref[pl.ds(lo, slab)] = jnp.zeros((slab, ny, nz), jnp.float32)
        pl.when(jnp.logical_not(inside(rel)))(clear)
    def chosen(devices):
        hit = own_slab == devices[0]
        for device in devices[1:]:
            hit = hit | (own_slab == device)
        return hit

    started = []
    for index, part, dest, lo, rel in copies:
        source = ins[index]
        if part == "orb":
            source = source.at[pl.ds(0, block_count)]
        elif part == "pot":
            source = source.at[block_count]
        if dest == "cells":
            target = cells_ref.at[:, pl.ds(lo, source.shape[1])]
        else:
            target = pot_ref.at[pl.ds(lo, source.shape[0])]
        copy = pltpu.make_async_copy(source, target, sems.at[len(started)])
        if rel is None:
            copy.start()
        else:
            pl.when(chosen(rel))(copy.start)
        started.append((copy, rel))
    def wait_for(kind):
        for (copy, rel), spec in zip(started, copies):
            if spec[2] != kind:
                continue
            if rel is None:
                copy.wait()
            else:
                pl.when(chosen(rel))(copy.wait)

    sources = (cells_ref,) + tuple(iter_refs)

    def plane_value(order, b, p):
        source = sources[order - 1]
        scale = 1.0 if order == 1 else 2.0
        field = source[b, RADIUS + p]
        total = zsum_ref[b, p]
        for offset, weight in enumerate(FOLDED, 1):
            beside_all = source[b, RADIUS + p + offset] + source[b, RADIUS + p - offset]
            beside_all = beside_all + pltpu.roll(field, offset, 0) + pltpu.roll(field, ny - offset, 0)
            total = total + (scale * weight) * beside_all
        total = total + potw_ref[min(order, 2) - 1, (order - 1) * RADIUS + p] * field
        if order == 1:
            return total
        return total - sources[order - 2][b, 2 * RADIUS + p]

    def along_z(order, planes):
        source = sources[order - 1]
        weights = cz_ref if order == 1 else cz2_ref
        for b in range(block_orbs):
            rows = source[b, RADIUS : RADIUS + planes].reshape(planes * ny, nz)
            mixed = jnp.dot(rows, weights[...], precision=lax.Precision.HIGHEST, preferred_element_type=jnp.float32)
            zsum_ref[b, :planes] = mixed.reshape(planes, ny, nz)

    def coefficients(q, carry):
        coefficient = (pot_ref[q] + FOLDED_SHIFT) * (1.0 / HALF_W)
        potw_ref[0, q] = coefficient
        potw_ref[1, q] = coefficient + coefficient
        return carry

    wait_for("cells")
    along_z(1, slab + 2 * (DEG_MAX - 1) * RADIUS)
    wait_for("pot")
    lax.fori_loop(0, pot_ref.shape[0], coefficients, 0)
    for order in range(1, DEG_MAX):
        margin = (DEG_MAX - order) * RADIUS
        dest = iter_refs[order - 1]
        planes = slab + 2 * margin
        if order > 1:
            along_z(order, planes)
        first_plane = first + order * RADIUS
        lo = jnp.minimum(jnp.maximum(-first_plane, 0), planes)
        hi = jnp.maximum(jnp.minimum(grid_planes - first_plane, planes), lo)
        for b in range(block_orbs):
            def clear(p, carry, b=b, dest=dest):
                dest[b, p] = jnp.zeros((ny, nz), jnp.float32)
                return carry

            def group(i, carry, order=order, b=b, dest=dest):
                for j in range(STEP):
                    dest[b, lo + STEP * i + j] = plane_value(order, b, lo + STEP * i + j)
                return carry

            def single(p, carry, order=order, b=b, dest=dest):
                dest[b, p] = plane_value(order, b, p)
                return carry

            lax.fori_loop(0, lo, clear, 0)
            lax.fori_loop(hi, planes, clear, 0)
            lax.fori_loop(0, (hi - lo) // STEP, group, 0)
            lax.fori_loop(lo + STEP * ((hi - lo) // STEP), hi, single, 0)

    along_z(DEG_MAX, slab)
    for b in range(block_orbs):
        def last(p, carry, b=b):
            value = plane_value(DEG_MAX, b, p)
            levels = jnp.full((ny, nz), degree, jnp.int32)
            picked = iter_refs[0][b, (DEG_MAX - 1) * RADIUS + p]
            for order in range(2, DEG_MAX):
                picked = jnp.where(levels >= order, iter_refs[order - 1][b, (DEG_MAX - order) * RADIUS + p], picked)
            picked = jnp.where(levels >= DEG_MAX, value, picked)
            out_ref[b, p] = picked.astype(out_ref.dtype)
            return carry
        lax.fori_loop(0, slab, last, 0, unroll=2)


def chebyshev_filter(orbitals, potential, first, degree, grid_planes):
    block_orbs, slab, ny, nz = orbitals.shape
    reach = DEG_MAX * RADIUS
    operands, copies, zeros = halo_plan(orbitals, potential, reach, reach - RADIUS)
    smem = pl.BlockSpec(memory_space=pltpu.SMEM)
    hbm = pl.BlockSpec(memory_space=pl.ANY)
    vmem = pl.BlockSpec(memory_space=pltpu.VMEM)
    return pl.pallas_call(
        functools.partial(
            filter_kernel,
            copies=tuple(copies),
            zeros=tuple(zeros),
            n_in=len(operands),
            block_count=block_orbs,
            grid_planes=grid_planes,
        ),
        out_shape=jax.ShapeDtypeStruct((block_orbs, slab, ny, nz), jnp.bfloat16),
        in_specs=[smem, smem, vmem, vmem, hbm, hbm] + [vmem] * (len(operands) - 2),
        out_specs=vmem,
        scratch_shapes=[
            pltpu.VMEM((block_orbs, slab + 2 * reach, ny, nz), jnp.float32),
            pltpu.VMEM((slab + 2 * (reach - RADIUS), ny, nz), jnp.float32),
            pltpu.VMEM((2, slab + 2 * (reach - RADIUS), ny, nz), jnp.float32),
            pltpu.VMEM((block_orbs, slab + 2 * (reach - RADIUS), ny, nz), jnp.float32),
            pltpu.SemaphoreType.DMA((len(copies),)),
        ]
        + [
            pltpu.VMEM((block_orbs, slab + 2 * (DEG_MAX - order) * RADIUS, ny, nz), jnp.float32)
            for order in range(1, DEG_MAX)
        ],
    )(first, degree, jnp.asarray(circulant(nz, 1.0)), jnp.asarray(circulant(nz, 2.0)), *operands)


def inner_rows(left, right):
    return lax.dot_general(
        left, right, (((1,), (1,)), ((), ())), preferred_element_type=jnp.float32
    )


def per_device(orbitals, potential, degrees):
    block_orbs, slab = orbitals.shape[0], orbitals.shape[1]
    n_orb, n_dom = lax.axis_size("orb"), lax.axis_size("dom")
    grid_planes = slab * n_dom
    start = lax.axis_index("dom") * slab
    first = (start - DEG_MAX * RADIUS).astype(jnp.int32).reshape(1)
    filtered = chebyshev_filter(orbitals, potential, first, degrees.astype(jnp.int32), grid_planes)
    cell_count = orbitals.shape[1] * orbitals.shape[2] * orbitals.shape[3]
    total_cells = float(cell_count * n_dom)
    flattened = filtered.reshape(block_orbs, cell_count)
    if n_orb & (n_orb - 1):
        mixed = lax.all_to_all(flattened, "orb", split_axis=1, concat_axis=0, tiled=True)
        partial_gram = inner_rows(mixed, mixed) / total_cells
    else:
        me = lax.axis_index("orb")
        shares = flattened.reshape(block_orbs, n_orb, -1)
        pieces = []
        for k in range(n_orb):
            share = lax.dynamic_index_in_dim(shares, jnp.bitwise_xor(me, k), axis=1, keepdims=False)
            pieces.append(share if k == 0 else lax.ppermute(share, "orb", [(i, i ^ k) for i in range(n_orb)]))
        mixed = jnp.concatenate(pieces, axis=0)
        by_partner = inner_rows(mixed, mixed) / total_cells
        row = jnp.arange(n_orb * block_orbs)
        order = jnp.bitwise_xor(row // block_orbs, me) * block_orbs + row % block_orbs
        partial_gram = by_partner[order][:, order]
    rows = partial_gram.reshape(n_orb, 1, block_orbs, -1)
    sends = jnp.broadcast_to(rows, (n_orb, n_dom) + rows.shape[2:]).reshape((n_orb * n_dom,) + rows.shape[2:])
    gathered = lax.all_to_all(sends, ("orb", "dom"), split_axis=0, concat_axis=0, tiled=True)
    correlation = gathered.sum(axis=0)
    return (filtered, correlation)


def solution(mesh):
    placed = (P("orb", "dom", None, None), P("dom", None, None), P("orb"))
    return jax.shard_map(
        per_device,
        mesh=mesh,
        in_specs=placed,
        out_specs=(P("orb", "dom", None, None), P("orb", None)),
        check_vma=False,
    )
```

```python
import functools

import numpy as np
import jax
import jax.numpy as jnp
from jax import lax
from jax.experimental import pallas as pl
from jax.experimental.pallas import tpu as pltpu
from jax.sharding import PartitionSpec as P

DEG_MAX = 3


CENTER_COEF = -5369.0 / 1800.0
STENCIL = (12.0 / 7.0, -15.0 / 56.0, 10.0 / 189.0, -1.0 / 112.0, 2.0 / 1925.0, -1.0 / 16632.0)
SHIFT_C = 8.5
HALF_W = 4.5
RADIUS = len(STENCIL)
STEP = 6
FOLDED = tuple(-0.5 * weight / HALF_W for weight in STENCIL)
FOLDED_SHIFT = -SHIFT_C - 1.5 * CENTER_COEF


def circulant(n, scale):
    gap = (np.arange(n)[None, :] - np.arange(n)[:, None]) % n
    weights = np.zeros((n, n), np.float32)
    for offset, weight in enumerate(FOLDED, 1):
        weights[(gap == offset) | (gap == n - offset)] = np.float32(scale * np.float32(weight))
    return weights


def shifted(x, k):
    count = lax.axis_size("dom")
    pairs = [(i, i + k) for i in range(count) if 0 <= i + k < count]
    if not pairs:
        return jnp.zeros_like(x)
    return lax.ppermute(x, "dom", pairs)


def gather_plan(orbitals, potential, reach, pot_reach):
    block_orbs, slab = orbitals.shape[0], orbitals.shape[1]
    count = lax.axis_size("dom")
    packed = jnp.concatenate([orbitals, potential[None]], axis=0)
    operands = [orbitals, potential]
    copies = [(0, "all", "cells", reach, None), (1, "all", "pot", pot_reach, None)]
    zeros = []
    pairwise = count & (count - 1) == 0
    for k in range(1, count):
        source = [j ^ k if pairwise else (j - k) % count for j in range(count)]
        near = [j for j in range(count) if abs(source[j] - j) * slab <= pot_reach]
        far = [j for j in range(count) if j not in near]
        for group, values, with_pot in ((near, packed, True), (far, orbitals, False)):
            if not group:
                continue
            operands.append(lax.ppermute(values, "dom", [(source[j], j) for j in group]))
            for rel in sorted({source[j] - j for j in group}):
                devices = tuple(j for j in group if source[j] - j == rel)
                copies.append((len(operands) - 1, "orb" if with_pot else "all", "cells", reach + rel * slab, devices))
                if with_pot:
                    copies.append((len(operands) - 1, "pot", "pot", pot_reach + rel * slab, devices))
    for rel in range(-(reach // slab), reach // slab + 1):
        if rel != 0:
            zeros.append(("cells", reach + rel * slab, rel))
            if abs(rel) * slab <= pot_reach:
                zeros.append(("pot", pot_reach + rel * slab, rel))
    return operands, copies, zeros


def halo_plan(orbitals, potential, reach, pot_reach):
    block_orbs, slab = orbitals.shape[0], orbitals.shape[1]
    if reach % slab == 0 and pot_reach % slab == 0 and lax.axis_size("dom") - 1 <= reach // slab:
        return gather_plan(orbitals, potential, reach, pot_reach)
    operands = [orbitals, potential]
    copies = [(0, "all", "cells", reach, None), (1, "all", "pot", pot_reach, None)]
    packed = None
    k = 1
    while slab * (k - 1) < reach:
        count = min(slab, reach - slab * (k - 1))
        pot_count = max(0, min(slab, pot_reach - slab * (k - 1)))
        for sign in (1, -1):
            if pot_count == slab and count == slab:
                if packed is None:
                    packed = jnp.concatenate([orbitals, potential[None]], axis=0)
                parts = [(packed, "orb", count, "cells", reach), (None, "pot", count, "pot", pot_reach)]
            else:
                parts = [(orbitals, "all", count, "cells", reach)]
                if pot_count:
                    parts.append((potential, "all", pot_count, "pot", pot_reach))
            for values, part, size, dest, centre in parts:
                lo = centre - slab * (k - 1) - size if sign > 0 else centre + slab * k
                if values is not None:
                    axis = 0 if values is potential else 1
                    span = values.shape[axis]
                    if sign > 0:
                        piece = lax.slice_in_dim(values, span - size, span, axis=axis)
                    else:
                        piece = lax.slice_in_dim(values, 0, size, axis=axis)
                    operands.append(shifted(piece, sign * k))
                copies.append((len(operands) - 1, part, dest, lo, None))
        k += 1
    return operands, copies, []


def filter_kernel(first_ref, deg_ref, cz_ref, cz2_ref, *refs, copies, zeros, n_in, block_count, grid_planes):
    ins = refs[:n_in]
    out_ref = refs[n_in]
    cells_ref, pot_ref, potw_ref, zsum_ref, sems = refs[n_in + 1 : n_in + 6]
    iter_refs = refs[n_in + 6 :]
    block_orbs, _, ny, nz = cells_ref.shape
    slab = out_ref.shape[1]
    first = first_ref[0]
    degree = deg_ref[0]

    reach = DEG_MAX * RADIUS
    own_slab = (first + reach) // slab

    def inside(rel):
        return (own_slab + rel >= 0) & (own_slab + rel < grid_planes // slab)

    for dest, lo, rel in zeros:
        def clear(dest=dest, lo=lo):
            if dest == "cells":
                cells_ref[:, pl.ds(lo, slab)] = jnp.zeros((block_orbs, slab, ny, nz), jnp.float32)
            else:
                pot_ref[pl.ds(lo, slab)] = jnp.zeros((slab, ny, nz), jnp.float32)
        pl.when(jnp.logical_not(inside(rel)))(clear)
    def chosen(devices):
        hit = own_slab == devices[0]
        for device in devices[1:]:
            hit = hit | (own_slab == device)
        return hit

    started = []
    for index, part, dest, lo, rel in copies:
        source = ins[index]
        if part == "orb":
            source = source.at[pl.ds(0, block_count)]
        elif part == "pot":
            source = source.at[block_count]
        if dest == "cells":
            target = cells_ref.at[:, pl.ds(lo, source.shape[1])]
        else:
            target = pot_ref.at[pl.ds(lo, source.shape[0])]
        copy = pltpu.make_async_copy(source, target, sems.at[len(started)])
        if rel is None:
            copy.start()
        else:
            pl.when(chosen(rel))(copy.start)
        started.append((copy, rel))
    def wait_for(kind):
        for (copy, rel), spec in zip(started, copies):
            if spec[2] != kind:
                continue
            if rel is None:
                copy.wait()
            else:
                pl.when(chosen(rel))(copy.wait)

    sources = (cells_ref,) + tuple(iter_refs)

    def plane_value(order, b, p):
        source = sources[order - 1]
        scale = 1.0 if order == 1 else 2.0
        field = source[b, RADIUS + p]
        total = zsum_ref[b, p]
        for offset, weight in enumerate(FOLDED, 1):
            beside_all = source[b, RADIUS + p + offset] + source[b, RADIUS + p - offset]
            beside_all = beside_all + pltpu.roll(field, offset, 0) + pltpu.roll(field, ny - offset, 0)
            total = total + (scale * weight) * beside_all
        total = total + potw_ref[min(order, 2) - 1, (order - 1) * RADIUS + p] * field
        if order == 1:
            return total
        return total - sources[order - 2][b, 2 * RADIUS + p]

    def along_z(order, planes):
        source = sources[order - 1]
        weights = cz_ref if order == 1 else cz2_ref
        for b in range(block_orbs):
            rows = source[b, RADIUS : RADIUS + planes].reshape(planes * ny, nz)
            mixed = jnp.dot(rows, weights[...], precision=lax.Precision.HIGHEST, preferred_element_type=jnp.float32)
            zsum_ref[b, :planes] = mixed.reshape(planes, ny, nz)

    def coefficients(q, carry):
        coefficient = (pot_ref[q] + FOLDED_SHIFT) * (1.0 / HALF_W)
        potw_ref[0, q] = coefficient
        potw_ref[1, q] = coefficient + coefficient
        return carry

    wait_for("cells")
    along_z(1, slab + 2 * (DEG_MAX - 1) * RADIUS)
    wait_for("pot")
    lax.fori_loop(0, pot_ref.shape[0], coefficients, 0, unroll=STEP)
    for order in range(1, DEG_MAX):
        margin = (DEG_MAX - order) * RADIUS
        dest = iter_refs[order - 1]
        planes = slab + 2 * margin
        if order > 1:
            along_z(order, planes)
        first_plane = first + order * RADIUS
        lo = jnp.minimum(jnp.maximum(-first_plane, 0), planes)
        hi = jnp.maximum(jnp.minimum(grid_planes - first_plane, planes), lo)
        for b in range(block_orbs):
            def clear(p, carry, b=b, dest=dest):
                dest[b, p] = jnp.zeros((ny, nz), jnp.float32)
                return carry

            def group(i, carry, order=order, b=b, dest=dest):
                for j in range(STEP):
                    dest[b, lo + STEP * i + j] = plane_value(order, b, lo + STEP * i + j)
                return carry

            def single(p, carry, order=order, b=b, dest=dest):
                dest[b, p] = plane_value(order, b, p)
                return carry

            lax.fori_loop(0, lo, clear, 0)
            lax.fori_loop(hi, planes, clear, 0)
            lax.fori_loop(0, (hi - lo) // STEP, group, 0)
            lax.fori_loop(lo + STEP * ((hi - lo) // STEP), hi, single, 0)

    along_z(DEG_MAX, slab)
    levels = jnp.full((ny, nz), degree, jnp.int32)
    for b in range(block_orbs):
        def last(p, carry, b=b):
            value = plane_value(DEG_MAX, b, p)
            picked = iter_refs[0][b, (DEG_MAX - 1) * RADIUS + p]
            for order in range(2, DEG_MAX):
                picked = jnp.where(levels >= order, iter_refs[order - 1][b, (DEG_MAX - order) * RADIUS + p], picked)
            picked = jnp.where(levels >= DEG_MAX, value, picked)
            out_ref[b, p] = picked.astype(out_ref.dtype)
            return carry
        lax.fori_loop(0, slab, last, 0, unroll=STEP)


def chebyshev_filter(orbitals, potential, first, degree, grid_planes):
    block_orbs, slab, ny, nz = orbitals.shape
    reach = DEG_MAX * RADIUS
    operands, copies, zeros = halo_plan(orbitals, potential, reach, reach - RADIUS)
    smem = pl.BlockSpec(memory_space=pltpu.SMEM)
    hbm = pl.BlockSpec(memory_space=pl.ANY)
    vmem = pl.BlockSpec(memory_space=pltpu.VMEM)
    return pl.pallas_call(
        functools.partial(
            filter_kernel,
            copies=tuple(copies),
            zeros=tuple(zeros),
            n_in=len(operands),
            block_count=block_orbs,
            grid_planes=grid_planes,
        ),
        out_shape=jax.ShapeDtypeStruct((block_orbs, slab, ny, nz), jnp.bfloat16),
        in_specs=[smem, smem, vmem, vmem, hbm, hbm] + [vmem] * (len(operands) - 2),
        out_specs=vmem,
        scratch_shapes=[
            pltpu.VMEM((block_orbs, slab + 2 * reach, ny, nz), jnp.float32),
            pltpu.VMEM((slab + 2 * (reach - RADIUS), ny, nz), jnp.float32),
            pltpu.VMEM((2, slab + 2 * (reach - RADIUS), ny, nz), jnp.float32),
            pltpu.VMEM((block_orbs, slab + 2 * (reach - RADIUS), ny, nz), jnp.float32),
            pltpu.SemaphoreType.DMA((len(copies),)),
        ]
        + [
            pltpu.VMEM((block_orbs, slab + 2 * (DEG_MAX - order) * RADIUS, ny, nz), jnp.float32)
            for order in range(1, DEG_MAX)
        ],
    )(first, degree, jnp.asarray(circulant(nz, 1.0)), jnp.asarray(circulant(nz, 2.0)), *operands)


def inner_rows(left, right):
    return lax.dot_general(
        left, right, (((1,), (1,)), ((), ())), preferred_element_type=jnp.float32
    )


def per_device(orbitals, potential, degrees):
    block_orbs, slab = orbitals.shape[0], orbitals.shape[1]
    n_orb, n_dom = lax.axis_size("orb"), lax.axis_size("dom")
    grid_planes = slab * n_dom
    start = lax.axis_index("dom") * slab
    first = (start - DEG_MAX * RADIUS).astype(jnp.int32).reshape(1)
    filtered = chebyshev_filter(orbitals, potential, first, degrees.astype(jnp.int32), grid_planes)
    cell_count = orbitals.shape[1] * orbitals.shape[2] * orbitals.shape[3]
    total_cells = float(cell_count * n_dom)
    flattened = filtered.reshape(block_orbs, cell_count)
    mixed = lax.all_to_all(flattened, "orb", split_axis=1, concat_axis=0, tiled=True)
    partial_gram = inner_rows(mixed, mixed) / total_cells
    rows = partial_gram.reshape(n_orb, 1, block_orbs, -1)
    sends = jnp.broadcast_to(rows, (n_orb, n_dom) + rows.shape[2:]).reshape((n_orb * n_dom,) + rows.shape[2:])
    gathered = lax.all_to_all(sends, ("orb", "dom"), split_axis=0, concat_axis=0, tiled=True)
    correlation = gathered.sum(axis=0)
    return (filtered, correlation)


def solution(mesh):
    placed = (P("orb", "dom", None, None), P("dom", None, None), P("orb"))
    return jax.shard_map(
        per_device,
        mesh=mesh,
        in_specs=placed,
        out_specs=(P("orb", "dom", None, None), P("orb", None)),
        check_vma=False,
    )
```

```python
import functools

import numpy as np
import jax
import jax.numpy as jnp
from jax import lax
from jax.experimental import pallas as pl
from jax.experimental.pallas import tpu as pltpu
from jax.sharding import PartitionSpec as P

DEG_MAX = 3


CENTER_COEF = -5369.0 / 1800.0
STENCIL = (12.0 / 7.0, -15.0 / 56.0, 10.0 / 189.0, -1.0 / 112.0, 2.0 / 1925.0, -1.0 / 16632.0)
SHIFT_C = 8.5
HALF_W = 4.5
RADIUS = len(STENCIL)
STEP = 6
FOLDED = tuple(-0.5 * weight / HALF_W for weight in STENCIL)
FOLDED_SHIFT = -SHIFT_C - 1.5 * CENTER_COEF


def circulant(n, scale):
    gap = (np.arange(n)[None, :] - np.arange(n)[:, None]) % n
    weights = np.zeros((n, n), np.float32)
    for offset, weight in enumerate(FOLDED, 1):
        weights[(gap == offset) | (gap == n - offset)] = np.float32(scale * np.float32(weight))
    return weights


def shifted(x, k):
    count = lax.axis_size("dom")
    pairs = [(i, i + k) for i in range(count) if 0 <= i + k < count]
    if not pairs:
        return jnp.zeros_like(x)
    return lax.ppermute(x, "dom", pairs)


def pack_kernel(orb_ref, pot_ref, out_ref, sems):
    block_orbs = orb_ref.shape[0]
    first = pltpu.make_async_copy(orb_ref, out_ref.at[pl.ds(0, block_orbs)], sems.at[0])
    second = pltpu.make_async_copy(pot_ref, out_ref.at[block_orbs], sems.at[1])
    first.start()
    second.start()
    first.wait()
    second.wait()


def packed_slab(orbitals, potential):
    block_orbs = orbitals.shape[0]
    hbm = pl.BlockSpec(memory_space=pl.ANY)
    return pl.pallas_call(
        pack_kernel,
        out_shape=jax.ShapeDtypeStruct((block_orbs + 1,) + orbitals.shape[1:], orbitals.dtype),
        in_specs=[hbm, hbm],
        out_specs=hbm,
        scratch_shapes=[pltpu.SemaphoreType.DMA((2,))],
    )(orbitals, potential)


def gather_plan(orbitals, potential, reach, pot_reach):
    block_orbs, slab = orbitals.shape[0], orbitals.shape[1]
    count = lax.axis_size("dom")
    packed = packed_slab(orbitals, potential)
    operands = [orbitals, potential]
    copies = [(0, "all", "cells", reach, None), (1, "all", "pot", pot_reach, None)]
    zeros = []
    pairwise = count & (count - 1) == 0
    for k in range(1, count):
        source = [j ^ k if pairwise else (j - k) % count for j in range(count)]
        near = [j for j in range(count) if abs(source[j] - j) * slab <= pot_reach]
        far = [j for j in range(count) if j not in near]
        for group, values, with_pot in ((near, packed, True), (far, orbitals, False)):
            if not group:
                continue
            operands.append(lax.ppermute(values, "dom", [(source[j], j) for j in group]))
            for rel in sorted({source[j] - j for j in group}):
                devices = tuple(j for j in group if source[j] - j == rel)
                copies.append((len(operands) - 1, "orb" if with_pot else "all", "cells", reach + rel * slab, devices))
                if with_pot:
                    copies.append((len(operands) - 1, "pot", "pot", pot_reach + rel * slab, devices))
    for rel in range(-(reach // slab), reach // slab + 1):
        if rel != 0:
            zeros.append(("cells", reach + rel * slab, rel))
            if abs(rel) * slab <= pot_reach:
                zeros.append(("pot", pot_reach + rel * slab, rel))
    return operands, copies, zeros


def halo_plan(orbitals, potential, reach, pot_reach):
    block_orbs, slab = orbitals.shape[0], orbitals.shape[1]
    if reach % slab == 0 and pot_reach % slab == 0 and lax.axis_size("dom") - 1 <= reach // slab:
        return gather_plan(orbitals, potential, reach, pot_reach)
    operands = [orbitals, potential]
    copies = [(0, "all", "cells", reach, None), (1, "all", "pot", pot_reach, None)]
    packed = None
    k = 1
    while slab * (k - 1) < reach:
        count = min(slab, reach - slab * (k - 1))
        pot_count = max(0, min(slab, pot_reach - slab * (k - 1)))
        for sign in (1, -1):
            if pot_count == slab and count == slab:
                if packed is None:
                    packed = jnp.concatenate([orbitals, potential[None]], axis=0)
                parts = [(packed, "orb", count, "cells", reach), (None, "pot", count, "pot", pot_reach)]
            else:
                parts = [(orbitals, "all", count, "cells", reach)]
                if pot_count:
                    parts.append((potential, "all", pot_count, "pot", pot_reach))
            for values, part, size, dest, centre in parts:
                lo = centre - slab * (k - 1) - size if sign > 0 else centre + slab * k
                if values is not None:
                    axis = 0 if values is potential else 1
                    span = values.shape[axis]
                    if sign > 0:
                        piece = lax.slice_in_dim(values, span - size, span, axis=axis)
                    else:
                        piece = lax.slice_in_dim(values, 0, size, axis=axis)
                    operands.append(shifted(piece, sign * k))
                copies.append((len(operands) - 1, part, dest, lo, None))
        k += 1
    return operands, copies, []


def filter_kernel(first_ref, deg_ref, cz_ref, cz2_ref, *refs, copies, zeros, n_in, block_count, grid_planes):
    ins = refs[:n_in]
    out_ref = refs[n_in]
    cells_ref, pot_ref, potw_ref, zsum_ref, sems = refs[n_in + 1 : n_in + 6]
    iter_refs = refs[n_in + 6 :]
    block_orbs, _, ny, nz = cells_ref.shape
    slab = out_ref.shape[1]
    first = first_ref[0]
    degree = deg_ref[0]

    reach = DEG_MAX * RADIUS
    own_slab = (first + reach) // slab

    def inside(rel):
        return (own_slab + rel >= 0) & (own_slab + rel < grid_planes // slab)

    for dest, lo, rel in zeros:
        def clear(dest=dest, lo=lo):
            if dest == "cells":
                cells_ref[:, pl.ds(lo, slab)] = jnp.zeros((block_orbs, slab, ny, nz), jnp.float32)
            else:
                pot_ref[pl.ds(lo, slab)] = jnp.zeros((slab, ny, nz), jnp.float32)
        pl.when(jnp.logical_not(inside(rel)))(clear)
    def chosen(devices):
        hit = own_slab == devices[0]
        for device in devices[1:]:
            hit = hit | (own_slab == device)
        return hit

    started = []
    for index, part, dest, lo, rel in copies:
        source = ins[index]
        if part == "orb":
            source = source.at[pl.ds(0, block_count)]
        elif part == "pot":
            source = source.at[block_count]
        if dest == "cells":
            target = cells_ref.at[:, pl.ds(lo, source.shape[1])]
        else:
            target = pot_ref.at[pl.ds(lo, source.shape[0])]
        copy = pltpu.make_async_copy(source, target, sems.at[len(started)])
        if rel is None:
            copy.start()
        else:
            pl.when(chosen(rel))(copy.start)
        started.append((copy, rel))
    def wait_for(kind):
        for (copy, rel), spec in zip(started, copies):
            if spec[2] != kind:
                continue
            if rel is None:
                copy.wait()
            else:
                pl.when(chosen(rel))(copy.wait)

    sources = (cells_ref,) + tuple(iter_refs)

    def plane_value(order, b, p):
        source = sources[order - 1]
        scale = 1.0 if order == 1 else 2.0
        field = source[b, RADIUS + p]
        total = zsum_ref[b, p]
        for offset, weight in enumerate(FOLDED, 1):
            beside_all = source[b, RADIUS + p + offset] + source[b, RADIUS + p - offset]
            beside_all = beside_all + pltpu.roll(field, offset, 0) + pltpu.roll(field, ny - offset, 0)
            total = total + (scale * weight) * beside_all
        total = total + potw_ref[min(order, 2) - 1, (order - 1) * RADIUS + p] * field
        if order == 1:
            return total
        return total - sources[order - 2][b, 2 * RADIUS + p]

    def along_z(order, planes):
        source = sources[order - 1]
        weights = cz_ref if order == 1 else cz2_ref
        for b in range(block_orbs):
            rows = source[b, RADIUS : RADIUS + planes].reshape(planes * ny, nz)
            mixed = jnp.dot(rows, weights[...], precision=lax.Precision.HIGHEST, preferred_element_type=jnp.float32)
            zsum_ref[b, :planes] = mixed.reshape(planes, ny, nz)

    def coefficients(q, carry):
        coefficient = (pot_ref[q] + FOLDED_SHIFT) * (1.0 / HALF_W)
        potw_ref[0, q] = coefficient
        potw_ref[1, q] = coefficient + coefficient
        return carry

    wait_for("cells")
    along_z(1, slab + 2 * (DEG_MAX - 1) * RADIUS)
    wait_for("pot")
    lax.fori_loop(0, pot_ref.shape[0], coefficients, 0, unroll=STEP)
    for order in range(1, DEG_MAX):
        margin = (DEG_MAX - order) * RADIUS
        dest = iter_refs[order - 1]
        planes = slab + 2 * margin
        if order > 1:
            along_z(order, planes)
        first_plane = first + order * RADIUS
        lo = jnp.minimum(jnp.maximum(-first_plane, 0), planes)
        hi = jnp.maximum(jnp.minimum(grid_planes - first_plane, planes), lo)
        for b in range(block_orbs):
            def clear(p, carry, b=b, dest=dest):
                dest[b, p] = jnp.zeros((ny, nz), jnp.float32)
                return carry

            def group(i, carry, order=order, b=b, dest=dest):
                for j in range(STEP):
                    dest[b, lo + STEP * i + j] = plane_value(order, b, lo + STEP * i + j)
                return carry

            def single(p, carry, order=order, b=b, dest=dest):
                dest[b, p] = plane_value(order, b, p)
                return carry

            lax.fori_loop(0, lo, clear, 0)
            lax.fori_loop(hi, planes, clear, 0)
            lax.fori_loop(0, (hi - lo) // STEP, group, 0)
            lax.fori_loop(lo + STEP * ((hi - lo) // STEP), hi, single, 0)

    along_z(DEG_MAX, slab)
    levels = jnp.full((ny, nz), degree, jnp.int32)
    for b in range(block_orbs):
        def last(p, carry, b=b):
            value = plane_value(DEG_MAX, b, p)
            picked = iter_refs[0][b, (DEG_MAX - 1) * RADIUS + p]
            for order in range(2, DEG_MAX):
                picked = jnp.where(levels >= order, iter_refs[order - 1][b, (DEG_MAX - order) * RADIUS + p], picked)
            picked = jnp.where(levels >= DEG_MAX, value, picked)
            out_ref[b, p] = picked.astype(out_ref.dtype)
            return carry
        lax.fori_loop(0, slab, last, 0, unroll=STEP)


def chebyshev_filter(orbitals, potential, first, degree, grid_planes):
    block_orbs, slab, ny, nz = orbitals.shape
    reach = DEG_MAX * RADIUS
    operands, copies, zeros = halo_plan(orbitals, potential, reach, reach - RADIUS)
    smem = pl.BlockSpec(memory_space=pltpu.SMEM)
    hbm = pl.BlockSpec(memory_space=pl.ANY)
    vmem = pl.BlockSpec(memory_space=pltpu.VMEM)
    return pl.pallas_call(
        functools.partial(
            filter_kernel,
            copies=tuple(copies),
            zeros=tuple(zeros),
            n_in=len(operands),
            block_count=block_orbs,
            grid_planes=grid_planes,
        ),
        out_shape=jax.ShapeDtypeStruct((block_orbs, slab, ny, nz), jnp.bfloat16),
        in_specs=[smem, smem, vmem, vmem, hbm, hbm] + [vmem] * (len(operands) - 2),
        out_specs=vmem,
        scratch_shapes=[
            pltpu.VMEM((block_orbs, slab + 2 * reach, ny, nz), jnp.float32),
            pltpu.VMEM((slab + 2 * (reach - RADIUS), ny, nz), jnp.float32),
            pltpu.VMEM((2, slab + 2 * (reach - RADIUS), ny, nz), jnp.float32),
            pltpu.VMEM((block_orbs, slab + 2 * (reach - RADIUS), ny, nz), jnp.float32),
            pltpu.SemaphoreType.DMA((len(copies),)),
        ]
        + [
            pltpu.VMEM((block_orbs, slab + 2 * (DEG_MAX - order) * RADIUS, ny, nz), jnp.float32)
            for order in range(1, DEG_MAX)
        ],
    )(first, degree, jnp.asarray(circulant(nz, 1.0)), jnp.asarray(circulant(nz, 2.0)), *operands)


def inner_rows(left, right):
    return lax.dot_general(
        left, right, (((1,), (1,)), ((), ())), preferred_element_type=jnp.float32
    )


def per_device(orbitals, potential, degrees):
    block_orbs, slab = orbitals.shape[0], orbitals.shape[1]
    n_orb, n_dom = lax.axis_size("orb"), lax.axis_size("dom")
    grid_planes = slab * n_dom
    start = lax.axis_index("dom") * slab
    first = (start - DEG_MAX * RADIUS).astype(jnp.int32).reshape(1)
    filtered = chebyshev_filter(orbitals, potential, first, degrees.astype(jnp.int32), grid_planes)
    cell_count = orbitals.shape[1] * orbitals.shape[2] * orbitals.shape[3]
    total_cells = float(cell_count * n_dom)
    flattened = filtered.reshape(block_orbs, cell_count)
    mixed = lax.all_to_all(flattened, "orb", split_axis=1, concat_axis=0, tiled=True)
    partial_gram = inner_rows(mixed, mixed) / total_cells
    rows = partial_gram.reshape(n_orb, 1, block_orbs, -1)
    sends = jnp.broadcast_to(rows, (n_orb, n_dom) + rows.shape[2:]).reshape((n_orb * n_dom,) + rows.shape[2:])
    gathered = lax.all_to_all(sends, ("orb", "dom"), split_axis=0, concat_axis=0, tiled=True)
    correlation = gathered.sum(axis=0)
    return (filtered, correlation)


def solution(mesh):
    placed = (P("orb", "dom", None, None), P("dom", None, None), P("orb"))
    return jax.shard_map(
        per_device,
        mesh=mesh,
        in_specs=placed,
        out_specs=(P("orb", "dom", None, None), P("orb", None)),
        check_vma=False,
    )
```

```python
import functools

import numpy as np
import jax
import jax.numpy as jnp
from jax import lax
from jax.experimental import pallas as pl
from jax.experimental.pallas import tpu as pltpu
from jax.sharding import PartitionSpec as P

DEG_MAX = 3


CENTER_COEF = -5369.0 / 1800.0
STENCIL = (12.0 / 7.0, -15.0 / 56.0, 10.0 / 189.0, -1.0 / 112.0, 2.0 / 1925.0, -1.0 / 16632.0)
SHIFT_C = 8.5
HALF_W = 4.5
RADIUS = len(STENCIL)
STEP = 6
FOLDED = tuple(-0.5 * weight / HALF_W for weight in STENCIL)
FOLDED_SHIFT = -SHIFT_C - 1.5 * CENTER_COEF


def circulant(n, scale):
    gap = (np.arange(n)[None, :] - np.arange(n)[:, None]) % n
    weights = np.zeros((n, n), np.float32)
    for offset, weight in enumerate(FOLDED, 1):
        weights[(gap == offset) | (gap == n - offset)] = np.float32(scale * np.float32(weight))
    return weights


def shifted(x, k):
    count = lax.axis_size("dom")
    pairs = [(i, i + k) for i in range(count) if 0 <= i + k < count]
    if not pairs:
        return jnp.zeros_like(x)
    return lax.ppermute(x, "dom", pairs)


def gather_plan(orbitals, potential, reach, pot_reach):
    block_orbs, slab = orbitals.shape[0], orbitals.shape[1]
    count = lax.axis_size("dom")
    packed = jnp.concatenate([orbitals, potential[None]], axis=0)
    operands = [orbitals, potential]
    copies = [(0, "all", "cells", reach, None), (1, "all", "pot", pot_reach, None)]
    zeros = []
    pairwise = count & (count - 1) == 0
    for k in range(1, count):
        source = [j ^ k if pairwise else (j - k) % count for j in range(count)]
        near = [j for j in range(count) if abs(source[j] - j) * slab <= pot_reach]
        far = [j for j in range(count) if j not in near]
        for group, values, with_pot in ((near, packed, True), (far, orbitals, False)):
            if not group:
                continue
            operands.append(lax.ppermute(values, "dom", [(source[j], j) for j in group]))
            for rel in sorted({source[j] - j for j in group}):
                devices = tuple(j for j in group if source[j] - j == rel)
                copies.append((len(operands) - 1, "orb" if with_pot else "all", "cells", reach + rel * slab, devices))
                if with_pot:
                    copies.append((len(operands) - 1, "pot", "pot", pot_reach + rel * slab, devices))
    for rel in range(-(reach // slab), reach // slab + 1):
        if rel != 0:
            zeros.append(("cells", reach + rel * slab, rel))
            if abs(rel) * slab <= pot_reach:
                zeros.append(("pot", pot_reach + rel * slab, rel))
    return operands, copies, zeros


def halo_plan(orbitals, potential, reach, pot_reach):
    block_orbs, slab = orbitals.shape[0], orbitals.shape[1]
    if reach % slab == 0 and pot_reach % slab == 0 and lax.axis_size("dom") - 1 <= reach // slab:
        return gather_plan(orbitals, potential, reach, pot_reach)
    operands = [orbitals, potential]
    copies = [(0, "all", "cells", reach, None), (1, "all", "pot", pot_reach, None)]
    packed = None
    k = 1
    while slab * (k - 1) < reach:
        count = min(slab, reach - slab * (k - 1))
        pot_count = max(0, min(slab, pot_reach - slab * (k - 1)))
        for sign in (1, -1):
            if pot_count == slab and count == slab:
                if packed is None:
                    packed = jnp.concatenate([orbitals, potential[None]], axis=0)
                parts = [(packed, "orb", count, "cells", reach), (None, "pot", count, "pot", pot_reach)]
            else:
                parts = [(orbitals, "all", count, "cells", reach)]
                if pot_count:
                    parts.append((potential, "all", pot_count, "pot", pot_reach))
            for values, part, size, dest, centre in parts:
                lo = centre - slab * (k - 1) - size if sign > 0 else centre + slab * k
                if values is not None:
                    axis = 0 if values is potential else 1
                    span = values.shape[axis]
                    if sign > 0:
                        piece = lax.slice_in_dim(values, span - size, span, axis=axis)
                    else:
                        piece = lax.slice_in_dim(values, 0, size, axis=axis)
                    operands.append(shifted(piece, sign * k))
                copies.append((len(operands) - 1, part, dest, lo, None))
        k += 1
    return operands, copies, []


def filter_kernel(first_ref, deg_ref, cz_ref, cz2_ref, *refs, copies, zeros, n_in, block_count, grid_planes):
    ins = refs[:n_in]
    out_ref = refs[n_in]
    cells_ref, pot_ref, potw_ref, zsum_ref, sems = refs[n_in + 1 : n_in + 6]
    iter_refs = refs[n_in + 6 :]
    block_orbs, _, ny, nz = cells_ref.shape
    slab = out_ref.shape[1]
    first = first_ref[0]
    degree = deg_ref[0]

    reach = DEG_MAX * RADIUS
    own_slab = (first + reach) // slab

    def inside(rel):
        return (own_slab + rel >= 0) & (own_slab + rel < grid_planes // slab)

    for dest, lo, rel in zeros:
        def clear(dest=dest, lo=lo):
            if dest == "cells":
                cells_ref[:, pl.ds(lo, slab)] = jnp.zeros((block_orbs, slab, ny, nz), jnp.float32)
            else:
                pot_ref[pl.ds(lo, slab)] = jnp.zeros((slab, ny, nz), jnp.float32)
        pl.when(jnp.logical_not(inside(rel)))(clear)
    def chosen(devices):
        hit = own_slab == devices[0]
        for device in devices[1:]:
            hit = hit | (own_slab == device)
        return hit

    started = []
    for index, part, dest, lo, rel in copies:
        source = ins[index]
        if part == "orb":
            source = source.at[pl.ds(0, block_count)]
        elif part == "pot":
            source = source.at[block_count]
        if dest == "cells":
            target = cells_ref.at[:, pl.ds(lo, source.shape[1])]
        else:
            target = pot_ref.at[pl.ds(lo, source.shape[0])]
        copy = pltpu.make_async_copy(source, target, sems.at[len(started)])
        if rel is None:
            copy.start()
        else:
            pl.when(chosen(rel))(copy.start)
        started.append((copy, rel))
    def wait_for(kind):
        for (copy, rel), spec in zip(started, copies):
            if spec[2] != kind:
                continue
            if rel is None:
                copy.wait()
            else:
                pl.when(chosen(rel))(copy.wait)

    sources = (cells_ref,) + tuple(iter_refs)

    def plane_value(order, b, p):
        source = sources[order - 1]
        scale = 1.0 if order == 1 else 2.0
        field = source[b, RADIUS + p]
        total = zsum_ref[b, p]
        for offset, weight in enumerate(FOLDED, 1):
            beside_all = source[b, RADIUS + p + offset] + source[b, RADIUS + p - offset]
            beside_all = beside_all + pltpu.roll(field, offset, 0) + pltpu.roll(field, ny - offset, 0)
            total = total + (scale * weight) * beside_all
        total = total + potw_ref[min(order, 2) - 1, (order - 1) * RADIUS + p] * field
        if order == 1:
            return total
        return total - sources[order - 2][b, 2 * RADIUS + p]

    def along_z(order, planes):
        source = sources[order - 1]
        weights = cz_ref if order == 1 else cz2_ref
        for b in range(block_orbs):
            rows = source[b, RADIUS : RADIUS + planes].reshape(planes * ny, nz)
            mixed = jnp.dot(rows, weights[...], precision=lax.Precision.HIGHEST, preferred_element_type=jnp.float32)
            zsum_ref[b, :planes] = mixed.reshape(planes, ny, nz)

    def coefficients(q, carry):
        coefficient = (pot_ref[q] + FOLDED_SHIFT) * (1.0 / HALF_W)
        potw_ref[0, q] = coefficient
        potw_ref[1, q] = coefficient + coefficient
        return carry

    wait_for("cells")
    along_z(1, slab + 2 * (DEG_MAX - 1) * RADIUS)
    wait_for("pot")
    lax.fori_loop(0, pot_ref.shape[0], coefficients, 0, unroll=STEP)
    for order in range(1, DEG_MAX):
        margin = (DEG_MAX - order) * RADIUS
        dest = iter_refs[order - 1]
        planes = slab + 2 * margin
        if order > 1:
            along_z(order, planes)
        first_plane = first + order * RADIUS
        lo = jnp.minimum(jnp.maximum(-first_plane, 0), planes)
        hi = jnp.maximum(jnp.minimum(grid_planes - first_plane, planes), lo)
        for b in range(block_orbs):
            def clear(p, carry, b=b, dest=dest):
                dest[b, p] = jnp.zeros((ny, nz), jnp.float32)
                return carry

            def group(i, carry, order=order, b=b, dest=dest, base=lo, step=2 * STEP):
                for j in range(step):
                    dest[b, base + step * i + j] = plane_value(order, b, base + step * i + j)
                return carry

            def half(i, carry, order=order, b=b, dest=dest, step=STEP):
                base = lo + 2 * STEP * ((hi - lo) // (2 * STEP))
                for j in range(step):
                    dest[b, base + step * i + j] = plane_value(order, b, base + step * i + j)
                return carry

            def single(p, carry, order=order, b=b, dest=dest):
                dest[b, p] = plane_value(order, b, p)
                return carry

            lax.fori_loop(0, lo, clear, 0)
            lax.fori_loop(hi, planes, clear, 0)
            lax.fori_loop(0, (hi - lo) // (2 * STEP), group, 0)
            rest = (hi - lo) % (2 * STEP)
            lax.fori_loop(0, rest // STEP, half, 0)
            lax.fori_loop(hi - rest % STEP, hi, single, 0)

    along_z(DEG_MAX, slab)
    levels = jnp.full((ny, nz), degree, jnp.int32)
    for b in range(block_orbs):
        def last(p, carry, b=b):
            value = plane_value(DEG_MAX, b, p)
            picked = iter_refs[0][b, (DEG_MAX - 1) * RADIUS + p]
            for order in range(2, DEG_MAX):
                picked = jnp.where(levels >= order, iter_refs[order - 1][b, (DEG_MAX - order) * RADIUS + p], picked)
            picked = jnp.where(levels >= DEG_MAX, value, picked)
            out_ref[b, p] = picked.astype(out_ref.dtype)
            return carry
        lax.fori_loop(0, slab, last, 0, unroll=STEP)


def chebyshev_filter(orbitals, potential, first, degree, grid_planes):
    block_orbs, slab, ny, nz = orbitals.shape
    reach = DEG_MAX * RADIUS
    operands, copies, zeros = halo_plan(orbitals, potential, reach, reach - RADIUS)
    smem = pl.BlockSpec(memory_space=pltpu.SMEM)
    hbm = pl.BlockSpec(memory_space=pl.ANY)
    vmem = pl.BlockSpec(memory_space=pltpu.VMEM)
    return pl.pallas_call(
        functools.partial(
            filter_kernel,
            copies=tuple(copies),
            zeros=tuple(zeros),
            n_in=len(operands),
            block_count=block_orbs,
            grid_planes=grid_planes,
        ),
        out_shape=jax.ShapeDtypeStruct((block_orbs, slab, ny, nz), jnp.bfloat16),
        in_specs=[smem, smem, vmem, vmem, hbm, hbm] + [vmem] * (len(operands) - 2),
        out_specs=vmem,
        scratch_shapes=[
            pltpu.VMEM((block_orbs, slab + 2 * reach, ny, nz), jnp.float32),
            pltpu.VMEM((slab + 2 * (reach - RADIUS), ny, nz), jnp.float32),
            pltpu.VMEM((2, slab + 2 * (reach - RADIUS), ny, nz), jnp.float32),
            pltpu.VMEM((block_orbs, slab + 2 * (reach - RADIUS), ny, nz), jnp.float32),
            pltpu.SemaphoreType.DMA((len(copies),)),
        ]
        + [
            pltpu.VMEM((block_orbs, slab + 2 * (DEG_MAX - order) * RADIUS, ny, nz), jnp.float32)
            for order in range(1, DEG_MAX)
        ],
    )(first, degree, jnp.asarray(circulant(nz, 1.0)), jnp.asarray(circulant(nz, 2.0)), *operands)


def inner_rows(left, right):
    return lax.dot_general(
        left, right, (((1,), (1,)), ((), ())), preferred_element_type=jnp.float32
    )


def per_device(orbitals, potential, degrees):
    block_orbs, slab = orbitals.shape[0], orbitals.shape[1]
    n_orb, n_dom = lax.axis_size("orb"), lax.axis_size("dom")
    grid_planes = slab * n_dom
    start = lax.axis_index("dom") * slab
    first = (start - DEG_MAX * RADIUS).astype(jnp.int32).reshape(1)
    filtered = chebyshev_filter(orbitals, potential, first, degrees.astype(jnp.int32), grid_planes)
    cell_count = orbitals.shape[1] * orbitals.shape[2] * orbitals.shape[3]
    total_cells = float(cell_count * n_dom)
    flattened = filtered.reshape(block_orbs, cell_count)
    mixed = lax.all_to_all(flattened, "orb", split_axis=1, concat_axis=0, tiled=True)
    partial_gram = inner_rows(mixed, mixed) / total_cells
    rows = partial_gram.reshape(n_orb, 1, block_orbs, -1)
    sends = jnp.broadcast_to(rows, (n_orb, n_dom) + rows.shape[2:]).reshape((n_orb * n_dom,) + rows.shape[2:])
    gathered = lax.all_to_all(sends, ("orb", "dom"), split_axis=0, concat_axis=0, tiled=True)
    correlation = gathered.sum(axis=0)
    return (filtered, correlation)


def solution(mesh):
    placed = (P("orb", "dom", None, None), P("dom", None, None), P("orb"))
    return jax.shard_map(
        per_device,
        mesh=mesh,
        in_specs=placed,
        out_specs=(P("orb", "dom", None, None), P("orb", None)),
        check_vma=False,
    )
```
